768 devices in a mesh: dom: 16 (over x, z_hi, core), sub: 48 (over z_lo, y).
Axes of the slice: x: 4, y: 8, z: 12 (z_hi: 2, z_lo: 6; z = z_hi * 6 + z_lo), core: 2. Of those that a mesh axis runs over, the one named last changes fastest.
Arguments:
- node_feat: bfloat16 [384, 1152, 128], P('dom', 'sub'), may hold values from -6 to 6
- edge_feat: bfloat16 [786432, 128], P(('dom', 'sub')), may hold values from -6 to 6
- edge_dst: int32 [786432], P(('dom', 'sub')), may hold values from 0 to 575
- edge_dir: int32 [786432], P(('dom', 'sub')), may hold values from 0 to 3, as said below
- edge_count: int32 [768], P(('dom', 'sub')), may hold values from 512 to 1024, as said below
- w_edge_in: bfloat16 [384, 128], P('dom'), may hold values from -0.3125 to 0.3125
- w_edge_out: bfloat16 [128, 128], P('dom'), may hold values from -0.5 to 0.5
- w_node_in: bfloat16 [256, 128], P('dom'), may hold values from -0.375 to 0.375
- w_node_out: bfloat16 [128, 128], P('dom'), may hold values from -0.5 to 0.5
- gains: bfloat16 [2, 128], P(None, 'dom'), may hold values from 0.099609375 to 1.8984375
- node_cot: bfloat16 [384, 1152, 128], P('dom', 'sub'), may hold values from -6 to 6
- edge_cot: bfloat16 [786432, 128], P(('dom', 'sub')), may hold values from -6 to 6
Outputs:
- node_grad: bfloat16 [384, 1152, 128], P('dom', 'sub')
- edge_grad: bfloat16 [786432, 128], P(('dom', 'sub'))
- w_edge_in_grad: float32 [384, 128], P('dom')
- w_edge_out_grad: float32 [128, 128], P('dom')
- w_node_in_grad: float32 [256, 128], P('dom')
- w_node_out_grad: float32 [128, 128], P('dom')
- gain_grad: float32 [2, 128], P(None, 'dom')
The draws below stay inside these ranges and needn't reach their ends.
Inputs may be any that keep to these rules, and one draw needn't show every extreme that they name: `edge_dir`: the sender lies inside the global grid. A device's live edges are its first edge_count slots; some device is full.
All inputs are finite; a program needn't handle non-finite values.
Results may differ from the reference program's by a relative error of at most 0.033.
The reference program's roundings to bfloat16 on the way count: a program that leaves them out, or rounds other values in their place, can miss the bound.
Values may be sent and summed in bfloat16 or wider, within the bound.
No kernel may reach another device: no remote copies, remote signals or barrier semaphores. Data moves between devices by JAX's collectives and lax.ppermute only.
A program may use at most 32 MiB of HBM per device.

```python
import jax
import jax.numpy as jnp
from jax import lax

F = 128
SIDE = 24
E_DEV = 1024
NX = 384
NY = 1152
NODES = 442368
EDGES = 786432
N_DOM = 16
N_SUB = 48


def edge_layout(key):
    base = jax.random.fold_in(key, 7)
    key_dst, key_dir = jax.random.split(base)
    target_local = jax.random.randint(key_dst, (EDGES,), 0, SIDE * SIDE, dtype=jnp.int32)
    drawn = jax.random.randint(key_dir, (EDGES,), 0, 4, dtype=jnp.int32)
    device = jnp.arange(EDGES, dtype=jnp.int32) // E_DEV
    columns_dev = NY // SIDE
    grid_row = device // columns_dev * SIDE + target_local // SIDE
    grid_col = device % columns_dev * SIDE + target_local % SIDE
    outside = (drawn == 0) & (grid_row == NX - 1) | (drawn == 1) & (grid_row == 0) | (drawn == 2) & (grid_col == NY - 1) | (drawn == 3) & (grid_col == 0)
    flipped = drawn + 1 - 2 * (drawn % 2)
    return (target_local, jnp.where(outside, flipped, drawn).astype(jnp.int32))


def draw_edge_dst(key, part):
    return edge_layout(key)[0]


def draw_edge_dir(key, part):
    return edge_layout(key)[1]


def draw_edge_count(key, part):
    devices = EDGES // E_DEV
    counts = jax.random.randint(jax.random.fold_in(key, 11), (devices,), E_DEV // 2, E_DEV + 1, dtype=jnp.int32)
    return counts.at[0].set(E_DEV)


def block_levels(own_key, dims, shards, low, largest):
    gain = 1.0
    for position, shards_of in shards:
        draws = jax.random.uniform(jax.random.fold_in(jax.random.fold_in(own_key, 6), position), (shards_of,), jnp.float32, low / len(shards), largest / len(shards))
        gain = gain * jnp.repeat(jnp.exp(draws), dims[position] // shards_of).reshape((-1,) + (1,) * (len(dims) - 1 - position))
    return gain


def centred(rng, extent, deviation, bound, shards=(), held_as=jnp.bfloat16):
    values = deviation * jax.random.normal(rng, extent, jnp.float32)
    if shards:
        values = values * block_levels(rng, extent, shards, -0.22, 0.18)
    return jnp.clip(values, -bound, bound).astype(held_as)


def setup_inputs(seed: int = 0) -> dict:
    key_of = jax.random.split(jax.random.key(seed), 13)
    node_feat = centred(key_of[0], (NX, NY, F), 1.0, 6.0, ((0, 16), (1, 48)))
    edge_feat = centred(key_of[1], (EDGES, F), 1.0, 6.0, ((0, 768),))
    edge_dst = draw_edge_dst(jax.random.fold_in(key_of[12], 71), 0)
    edge_dir = draw_edge_dir(jax.random.fold_in(key_of[12], 71), 0)
    edge_count = draw_edge_count(jax.random.fold_in(key_of[12], 71), 0)
    w_edge_in = centred(key_of[5], (3 * F, F), (3 * F) ** -0.5, 0.3125, ((0, 16),))
    w_edge_out = centred(key_of[6], (F, F), F ** -0.5, 0.5, ((0, 16),))
    w_node_in = centred(key_of[7], (2 * F, F), (2 * F) ** -0.5, 0.375, ((0, 16),))
    w_node_out = centred(key_of[8], (F, F), F ** -0.5, 0.5, ((0, 16),))
    gains = jnp.clip(1.0 + 0.18 * jax.random.normal(key_of[9], (2, F), jnp.float32), 0.099609375, 1.8984375).astype(jnp.bfloat16)
    node_cot = centred(key_of[10], (NX, NY, F), 1.0, 6.0, ((0, 16), (1, 48)))
    edge_cot = centred(key_of[11], (EDGES, F), 1.0, 6.0, ((0, 768),))
    return {"node_feat": node_feat, "edge_feat": edge_feat, "edge_dst": edge_dst, "edge_dir": edge_dir, "edge_count": edge_count, "w_edge_in": w_edge_in, "w_edge_out": w_edge_out, "w_node_in": w_node_in, "w_node_out": w_node_out, "gains": gains, "node_cot": node_cot, "edge_cot": edge_cot}


def layer_norm(raw_out):
    average = lax.optimization_barrier(jnp.mean(raw_out, axis=-1, keepdims=True))
    centered = raw_out - average
    inv_std = lax.rsqrt(lax.optimization_barrier(jnp.mean(centered * centered, axis=-1, keepdims=True)) + 1e-05)
    return (centered * inv_std, inv_std)

def norm_back(upstream, normed, inv_std):
    return (upstream - lax.optimization_barrier(jnp.mean(upstream, axis=-1, keepdims=True)) - normed * lax.optimization_barrier(jnp.mean(upstream * normed, axis=-1, keepdims=True))) * inv_std

def mlp_forward(inputs, w_first, w_second, gain_vec):
    pre_act = jnp.dot(inputs, w_first, preferred_element_type=jnp.float32)
    hidden = jnp.maximum(pre_act, 0.0).astype(jnp.bfloat16)
    raw_out = jnp.dot(hidden, w_second, preferred_element_type=jnp.float32)
    normed, inv_std = layer_norm(raw_out)
    return (pre_act, hidden, normed, inv_std, normed * gain_vec)

def mlp_backward(upstream, inputs, pre_act, hidden, normed, inv_std, gain_vec, w_first, w_second):
    gain_part = lax.optimization_barrier(jnp.sum(upstream * normed, axis=0))
    grad_raw = norm_back(upstream * gain_vec, normed, inv_std).astype(jnp.bfloat16)
    second_part = jnp.dot(hidden.T, grad_raw, preferred_element_type=jnp.float32)
    grad_hidden = jnp.dot(grad_raw, w_second.T, preferred_element_type=jnp.float32)
    grad_pre = jnp.where(pre_act > 0, grad_hidden, 0.0).astype(jnp.bfloat16)
    first_part = jnp.dot(inputs.T, grad_pre, preferred_element_type=jnp.float32)
    grad_inputs = jnp.dot(grad_pre, w_first.T, preferred_element_type=jnp.float32)
    return (grad_inputs, first_part, second_part, gain_part)

def reference(node_feat, edge_feat, edge_dst, edge_dir, edge_count, w_edge_in, w_edge_out, w_node_in, w_node_out, gains, node_cot, edge_cot):
    devices = N_DOM * N_SUB
    node_rows = node_feat.reshape(NODES, F)
    gain_edge = gains[0].astype(jnp.float32)
    gain_node = gains[1].astype(jnp.float32)
    feat_blocks = edge_feat.reshape(devices, E_DEV, F)
    cot_blocks = edge_cot.reshape(devices, E_DEV, F)
    dst_blocks = edge_dst.reshape(devices, E_DEV)
    dir_blocks = edge_dir.reshape(devices, E_DEV)
    device_ids = jnp.arange(devices, dtype=jnp.int32)

    def locate(target_local, direction, device):
        grid_row = device // N_SUB * SIDE + target_local // SIDE
        grid_col = device % N_SUB * SIDE + target_local % SIDE
        step_row = jnp.where(direction == 0, 1, jnp.where(direction == 1, -1, 0)).astype(jnp.int32)
        step_col = jnp.where(direction == 2, 1, jnp.where(direction == 3, -1, 0)).astype(jnp.int32)
        active = (jnp.arange(E_DEV, dtype=jnp.int32) < edge_count[device]).astype(jnp.float32)[:, None]
        target = (grid_row * NY + grid_col).astype(jnp.int32)
        source = ((grid_row + step_row) * NY + grid_col + step_col).astype(jnp.int32)
        return (target, source, active)

    def aggregate_pass(totals, blocks):
        features, target_local, direction, device = blocks
        target, source, active = locate(target_local, direction, device)
        inputs = jnp.concatenate([features, node_rows[source], node_rows[target]], axis=1)
        message = mlp_forward(inputs, w_edge_in, w_edge_out, gain_edge)[4]
        return (totals.at[target].add(message * active), None)
    aggregate, _ = lax.scan(aggregate_pass, jnp.zeros((NODES, F), jnp.float32), (feat_blocks, dst_blocks, dir_blocks, device_ids))
    node_input = jnp.concatenate([node_rows, aggregate.astype(jnp.bfloat16)], axis=1)
    pre_act, hidden, normed, inv_std, _ = mlp_forward(node_input, w_node_in, w_node_out, gain_node)
    node_upstream = node_cot.reshape(NODES, F).astype(jnp.float32)
    node_in_grad, node_first, node_second, node_gain = mlp_backward(node_upstream, node_input, pre_act, hidden, normed, inv_std, gain_node, w_node_in, w_node_out)
    agg_grad = node_in_grad[:, F:]

    def second(totals, blocks):
        spread_grad, first_sum, second_sum, gain_sum = totals
        features, cotangent, target_local, direction, device = blocks
        target, source, active = locate(target_local, direction, device)
        inputs = jnp.concatenate([features, node_rows[source], node_rows[target]], axis=1)
        pre_e, hidden_e, normed_e, inv_e, _ = mlp_forward(inputs, w_edge_in, w_edge_out, gain_edge)
        cot_float = cotangent.astype(jnp.float32)
        upstream = active * (cot_float + agg_grad[target])
        edge_in_grad, first_part, second_part, gain_part = mlp_backward(upstream, inputs, pre_e, hidden_e, normed_e, inv_e, gain_edge, w_edge_in, w_edge_out)
        edge_out = (cot_float + edge_in_grad[:, :F]).astype(jnp.bfloat16)
        spread_grad = spread_grad.at[source].add(edge_in_grad[:, F:2 * F]).at[target].add(edge_in_grad[:, 2 * F:])
        return ((spread_grad, first_sum + first_part, second_sum + second_part, gain_sum + gain_part), edge_out)
    start = (jnp.zeros((NODES, F), jnp.float32), jnp.zeros((3 * F, F), jnp.float32), jnp.zeros((F, F), jnp.float32), jnp.zeros((F,), jnp.float32))
    totals, edge_out = lax.scan(second, start, (feat_blocks, cot_blocks, dst_blocks, dir_blocks, device_ids))
    spread_grad, edge_first, edge_second, edge_gain = totals
    node_grad = (node_upstream + node_in_grad[:, :F] + spread_grad).astype(jnp.bfloat16).reshape(NX, NY, F)
    grad_scale = lax.rsqrt(jnp.float32(NODES))
    gain_grad = jnp.stack([edge_gain, node_gain]) * grad_scale
    return (node_grad, edge_out.reshape(EDGES, F), edge_first * grad_scale, edge_second * grad_scale, node_first * grad_scale, node_second * grad_scale, gain_grad)
```

```python
import jax
import jax.numpy as jnp
from jax import lax
from jax.sharding import PartitionSpec as P


def with_halo(block, sides, width):
    for axis, dim in sides:
        count = lax.axis_size(axis)
        forward = [(i, i + 1) for i in range(count - 1)]
        backward = [(target, source) for source, target in forward]
        low = lax.ppermute(
            lax.slice_in_dim(block, block.shape[dim] - width, None, axis=dim), axis, forward
        )
        high = lax.ppermute(lax.slice_in_dim(block, 0, width, axis=dim), axis, backward)
        block = jnp.concatenate([low, block, high], axis=dim)
    return block


def layer_norm(raw_out):
    average = jnp.mean(raw_out, axis=-1, keepdims=True)
    centered = raw_out - average
    inv_std = lax.rsqrt(jnp.mean(centered * centered, axis=-1, keepdims=True) + 1e-05)
    return (centered * inv_std, inv_std)


def norm_back(upstream, normed, inv_std):
    return (
        upstream
        - jnp.mean(upstream, axis=-1, keepdims=True)
        - normed * jnp.mean(upstream * normed, axis=-1, keepdims=True)
    ) * inv_std


def mlp_forward(inputs, w_first, w_second, gain_vec):
    pre_act = jnp.dot(inputs, w_first, preferred_element_type=jnp.float32)
    hidden = jnp.maximum(pre_act, 0.0).astype(jnp.bfloat16)
    raw_out = jnp.dot(hidden, w_second, preferred_element_type=jnp.float32)
    normed, inv_std = layer_norm(raw_out)
    return (pre_act, hidden, normed, inv_std, normed * gain_vec)


def mlp_backward(upstream, inputs, pre_act, hidden, normed, inv_std, gain_vec, w_first, w_second):
    gain_part = jnp.sum(upstream * normed, axis=0)
    grad_raw = norm_back(upstream * gain_vec, normed, inv_std).astype(jnp.bfloat16)
    second_part = jnp.dot(hidden.T, grad_raw, preferred_element_type=jnp.float32)
    grad_hidden = jnp.dot(grad_raw, w_second.T, preferred_element_type=jnp.float32)
    grad_pre = jnp.where(pre_act > 0, grad_hidden, 0.0).astype(jnp.bfloat16)
    first_part = jnp.dot(inputs.T, grad_pre, preferred_element_type=jnp.float32)
    grad_inputs = jnp.dot(grad_pre, w_first.T, preferred_element_type=jnp.float32)
    return (grad_inputs, first_part, second_part, gain_part)


def gather_params(weights, gains):
    latent = weights[0].shape[1]
    gain_row = gains.reshape(1, -1)
    gain_row = jnp.pad(gain_row, ((0, 0), (0, latent - gain_row.shape[1])))
    packed = jnp.concatenate(list(weights) + [gain_row], axis=0)
    full = lax.all_gather(packed, "dom", axis=0, tiled=False)
    count = full.shape[0]
    outs = []
    start = 0
    for w in weights:
        rows = w.shape[0]
        outs.append(full[:, start : start + rows].reshape(count * rows, latent))
        start += rows
    width = gains.shape[1]
    gain_full = full[:, start, : 2 * width].reshape(count, 2, width)
    gain_full = jnp.transpose(gain_full, (1, 0, 2)).reshape(2, count * width)
    outs.append(gain_full)
    return tuple(outs)


def reduce_params(parts, gain_terms, scale):
    count = lax.axis_size("dom")
    latent = parts[0].shape[1]
    blocks = [p.reshape(count, p.shape[0] // count, latent) for p in parts]
    width = gain_terms.shape[1] // count
    gain_block = jnp.transpose(gain_terms.reshape(2, count, width), (1, 0, 2)).reshape(count, 1, 2 * width)
    gain_block = jnp.pad(gain_block, ((0, 0), (0, 0), (0, latent - 2 * width)))
    packed = jnp.concatenate(blocks + [gain_block], axis=1)
    shard = lax.psum_scatter(packed, "dom", scatter_dimension=0, tiled=True)[0]
    shard = lax.psum(shard, "sub") * scale
    outs = []
    start = 0
    for b in blocks:
        rows = b.shape[1]
        outs.append(shard[start : start + rows])
        start += rows
    outs.append(shard[start, : 2 * width].reshape(2, width))
    return tuple(outs)


def shards(
    node_feat,
    edge_feat,
    edge_dst,
    edge_dir,
    edge_count,
    w_edge_in,
    w_edge_out,
    w_node_in,
    w_node_out,
    gains,
    node_cot,
    edge_cot,
):
    full_edge_in, full_edge_out, full_node_in, full_node_out, full_gains = gather_params(
        (w_edge_in, w_edge_out, w_node_in, w_node_out), gains
    )
    gain_edge = full_gains[0].astype(jnp.float32)
    gain_node = full_gains[1].astype(jnp.float32)
    block_side = node_feat.shape[0]
    latent = node_feat.shape[2]
    padded_side = block_side + 2
    padded = with_halo(node_feat, (("dom", 0), ("sub", 1)), 1).reshape(
        padded_side * padded_side, latent
    )
    node_row = edge_dst // block_side
    node_col = edge_dst % block_side
    step_row = jnp.where(edge_dir == 0, 1, jnp.where(edge_dir == 1, -1, 0)).astype(jnp.int32)
    step_col = jnp.where(edge_dir == 2, 1, jnp.where(edge_dir == 3, -1, 0)).astype(jnp.int32)
    target_pad = (node_row + 1) * padded_side + node_col + 1
    source_pad = (node_row + 1 + step_row) * padded_side + node_col + 1 + step_col
    active = (jnp.arange(edge_dst.shape[0], dtype=jnp.int32) < edge_count[0]).astype(jnp.float32)[
        :, None
    ]
    inputs = jnp.concatenate([edge_feat, padded[source_pad], padded[target_pad]], axis=1)
    pre_e, hidden_e, normed_e, inv_e, message = mlp_forward(
        inputs, full_edge_in, full_edge_out, gain_edge
    )
    aggregate = jax.ops.segment_sum(
        message * active, edge_dst, num_segments=block_side * block_side
    )
    node_rows = node_feat.reshape(block_side * block_side, latent)
    node_input = jnp.concatenate([node_rows, aggregate.astype(jnp.bfloat16)], axis=1)
    pre_n, hidden_n, normed_n, inv_n, _ = mlp_forward(
        node_input, full_node_in, full_node_out, gain_node
    )
    node_upstream = node_cot.reshape(block_side * block_side, latent).astype(jnp.float32)
    node_in_grad, node_first, node_second, node_gain = mlp_backward(
        node_upstream,
        node_input,
        pre_n,
        hidden_n,
        normed_n,
        inv_n,
        gain_node,
        full_node_in,
        full_node_out,
    )
    cot_float = edge_cot.astype(jnp.float32)
    upstream = active * (cot_float + node_in_grad[:, latent:][edge_dst])
    edge_in_grad, edge_first, edge_second, edge_gain = mlp_backward(
        upstream, inputs, pre_e, hidden_e, normed_e, inv_e, gain_edge, full_edge_in, full_edge_out
    )
    edge_grad = (cot_float + edge_in_grad[:, :latent]).astype(jnp.bfloat16)
    spread = jnp.zeros((padded_side * padded_side, latent), jnp.float32)
    spread = (
        spread.at[source_pad]
        .add(edge_in_grad[:, latent : 2 * latent])
        .at[target_pad]
        .add(edge_in_grad[:, 2 * latent :])
    )
    spread = spread.reshape(padded_side, padded_side, latent)
    outgoing = jnp.stack(
        [
            jnp.stack([spread[1:-1, 0], spread[0, 1:-1]]),
            jnp.stack([spread[-1, 1:-1], spread[1:-1, -1]]),
        ]
    )
    incoming = with_halo(outgoing.astype(jnp.bfloat16), (("dom", 0), ("sub", 1)), 1).astype(
        outgoing.dtype
    )
    inner = spread[1:-1, 1:-1]
    inner = inner.at[0].add(incoming[0, 1]).at[-1].add(incoming[3, 2])
    inner = inner.at[:, 0].add(incoming[2, 0]).at[:, -1].add(incoming[1, 3])
    node_total = node_upstream + node_in_grad[:, :latent]
    node_grad = (node_total.reshape(block_side, block_side, latent) + inner).astype(jnp.bfloat16)
    nodes_all = block_side * block_side * lax.axis_size("dom") * lax.axis_size("sub")
    grad_scale = lax.rsqrt(jnp.float32(nodes_all))
    results = reduce_params(
        (edge_first, edge_second, node_first, node_second), jnp.stack([edge_gain, node_gain]), grad_scale
    )
    return (node_grad, edge_grad) + results


def solution(mesh):
    in_specs = (
        P("dom", "sub", None),
        P(("dom", "sub"), None),
        P(("dom", "sub")),
        P(("dom", "sub")),
        P(("dom", "sub")),
        P("dom", None),
        P("dom", None),
        P("dom", None),
        P("dom", None),
        P(None, "dom"),
        P("dom", "sub", None),
        P(("dom", "sub"), None),
    )
    out_specs = (
        P("dom", "sub", None),
        P(("dom", "sub"), None),
        P("dom", None),
        P("dom", None),
        P("dom", None),
        P("dom", None),
        P(None, "dom"),
    )
    return jax.shard_map(shards, mesh=mesh, in_specs=in_specs, out_specs=out_specs, check_vma=False)
```

```python
import jax
import jax.numpy as jnp
from jax import lax
from jax.sharding import PartitionSpec as P


def with_halo(block, sides, width):
    for axis, dim in sides:
        count = lax.axis_size(axis)
        forward = [(i, i + 1) for i in range(count - 1)]
        backward = [(target, source) for source, target in forward]
        low = lax.ppermute(
            lax.slice_in_dim(block, block.shape[dim] - width, None, axis=dim), axis, forward
        )
        high = lax.ppermute(lax.slice_in_dim(block, 0, width, axis=dim), axis, backward)
        block = jnp.concatenate([low, block, high], axis=dim)
    return block


def layer_norm(raw_out):
    average = jnp.mean(raw_out, axis=-1, keepdims=True)
    centered = raw_out - average
    inv_std = lax.rsqrt(jnp.mean(centered * centered, axis=-1, keepdims=True) + 1e-05)
    return (centered * inv_std, inv_std)


def norm_back(upstream, normed, inv_std):
    return (
        upstream
        - jnp.mean(upstream, axis=-1, keepdims=True)
        - normed * jnp.mean(upstream * normed, axis=-1, keepdims=True)
    ) * inv_std


def mlp_forward(inputs, w_first, w_second, gain_vec):
    pre_act = jnp.dot(inputs, w_first, preferred_element_type=jnp.float32)
    hidden = jnp.maximum(pre_act, 0.0).astype(jnp.bfloat16)
    raw_out = jnp.dot(hidden, w_second, preferred_element_type=jnp.float32)
    normed, inv_std = layer_norm(raw_out)
    return (pre_act, hidden, normed, inv_std, normed * gain_vec)


def mlp_backward(upstream, inputs, pre_act, hidden, normed, inv_std, gain_vec, w_first, w_second):
    gain_part = jnp.sum(upstream * normed, axis=0)
    grad_raw = norm_back(upstream * gain_vec, normed, inv_std).astype(jnp.bfloat16)
    second_part = jnp.dot(hidden.T, grad_raw, preferred_element_type=jnp.float32)
    grad_hidden = jnp.dot(grad_raw, w_second.T, preferred_element_type=jnp.float32)
    grad_pre = jnp.where(pre_act > 0, grad_hidden, 0.0).astype(jnp.bfloat16)
    first_part = jnp.dot(inputs.T, grad_pre, preferred_element_type=jnp.float32)
    grad_inputs = jnp.dot(grad_pre, w_first.T, preferred_element_type=jnp.float32)
    return (grad_inputs, first_part, second_part, gain_part)


def exchange(value, axis, mask):
    count = lax.axis_size(axis)
    return lax.ppermute(value, axis, [(i, i ^ mask) for i in range(count)])


def bit_masks(count):
    masks = []
    mask = 1
    while mask < count:
        masks.append(mask)
        mask *= 2
    return masks


def gather_dom(packed):
    index = lax.axis_index("dom")
    block = packed
    for mask in bit_masks(lax.axis_size("dom")):
        other = exchange(block, "dom", mask)
        low = (index & mask) == 0
        block = jnp.where(low, jnp.stack([block, other]), jnp.stack([other, block]))
    return block.reshape((-1,) + packed.shape)


def reduce_scatter_dom(packed):
    count = lax.axis_size("dom")
    index = lax.axis_index("dom")
    masks = bit_masks(count)
    block = packed.reshape((2,) * len(masks) + packed.shape[1:])
    for position, mask in enumerate(reversed(masks)):
        low_half = block[0]
        high_half = block[1]
        low = (index & mask) == 0
        keep = jnp.where(low, low_half, high_half)
        send = jnp.where(low, high_half, low_half)
        block = keep + exchange(send, "dom", mask)
    return block


def sum_sub(value):
    count = lax.axis_size("sub")
    index = lax.axis_index("sub")
    total = value
    mask = 1
    while count % (2 * mask) == 0:
        total = total + exchange(total, "sub", mask)
        mask *= 2
    rest = count // mask
    if rest > 1:
        member = index // mask
        shifted = [total] + [
            lax.ppermute(total, "sub", [(i, (i + k * mask) % count) for i in range(count)])
            for k in range(1, rest)
        ]
        stacked = jnp.stack(shifted)
        ordered = lax.dynamic_index_in_dim(stacked, member % rest, keepdims=False)
        for source in range(1, rest):
            pick = (member - source) % rest
            ordered = ordered + lax.dynamic_index_in_dim(stacked, pick, keepdims=False)
        total = ordered
    return total


def gather_params(weights, gains):
    latent = weights[0].shape[1]
    gain_row = gains.reshape(1, -1)
    gain_row = jnp.pad(gain_row, ((0, 0), (0, latent - gain_row.shape[1])))
    packed = jnp.concatenate(list(weights) + [gain_row], axis=0)
    full = gather_dom(packed)
    count = full.shape[0]
    outs = []
    start = 0
    for w in weights:
        rows = w.shape[0]
        outs.append(full[:, start : start + rows].reshape(count * rows, latent))
        start += rows
    width = gains.shape[1]
    gain_full = full[:, start, : 2 * width].reshape(count, 2, width)
    gain_full = jnp.transpose(gain_full, (1, 0, 2)).reshape(2, count * width)
    outs.append(gain_full)
    return tuple(outs)


def reduce_params(parts, gain_terms, scale):
    count = lax.axis_size("dom")
    latent = parts[0].shape[1]
    blocks = [p.reshape(count, p.shape[0] // count, latent) for p in parts]
    width = gain_terms.shape[1] // count
    gain_block = jnp.transpose(gain_terms.reshape(2, count, width), (1, 0, 2)).reshape(count, 1, 2 * width)
    gain_block = jnp.pad(gain_block, ((0, 0), (0, 0), (0, latent - 2 * width)))
    packed = jnp.concatenate(blocks + [gain_block], axis=1)
    shard = reduce_scatter_dom(packed)
    shard = sum_sub(shard) * scale
    outs = []
    start = 0
    for b in blocks:
        rows = b.shape[1]
        outs.append(shard[start : start + rows])
        start += rows
    outs.append(shard[start, : 2 * width].reshape(2, width))
    return tuple(outs)


def shards(
    node_feat,
    edge_feat,
    edge_dst,
    edge_dir,
    edge_count,
    w_edge_in,
    w_edge_out,
    w_node_in,
    w_node_out,
    gains,
    node_cot,
    edge_cot,
):
    full_edge_in, full_edge_out, full_node_in, full_node_out, full_gains = gather_params(
        (w_edge_in, w_edge_out, w_node_in, w_node_out), gains
    )
    gain_edge = full_gains[0].astype(jnp.float32)
    gain_node = full_gains[1].astype(jnp.float32)
    block_side = node_feat.shape[0]
    latent = node_feat.shape[2]
    padded_side = block_side + 2
    padded = with_halo(node_feat, (("dom", 0), ("sub", 1)), 1).reshape(
        padded_side * padded_side, latent
    )
    node_row = edge_dst // block_side
    node_col = edge_dst % block_side
    step_row = jnp.where(edge_dir == 0, 1, jnp.where(edge_dir == 1, -1, 0)).astype(jnp.int32)
    step_col = jnp.where(edge_dir == 2, 1, jnp.where(edge_dir == 3, -1, 0)).astype(jnp.int32)
    target_pad = (node_row + 1) * padded_side + node_col + 1
    source_pad = (node_row + 1 + step_row) * padded_side + node_col + 1 + step_col
    active = (jnp.arange(edge_dst.shape[0], dtype=jnp.int32) < edge_count[0]).astype(jnp.float32)[
        :, None
    ]
    inputs = jnp.concatenate([edge_feat, padded[source_pad], padded[target_pad]], axis=1)
    pre_e, hidden_e, normed_e, inv_e, message = mlp_forward(
        inputs, full_edge_in, full_edge_out, gain_edge
    )
    aggregate = jax.ops.segment_sum(
        message * active, edge_dst, num_segments=block_side * block_side
    )
    node_rows = node_feat.reshape(block_side * block_side, latent)
    node_input = jnp.concatenate([node_rows, aggregate.astype(jnp.bfloat16)], axis=1)
    pre_n, hidden_n, normed_n, inv_n, _ = mlp_forward(
        node_input, full_node_in, full_node_out, gain_node
    )
    node_upstream = node_cot.reshape(block_side * block_side, latent).astype(jnp.float32)
    node_in_grad, node_first, node_second, node_gain = mlp_backward(
        node_upstream,
        node_input,
        pre_n,
        hidden_n,
        normed_n,
        inv_n,
        gain_node,
        full_node_in,
        full_node_out,
    )
    cot_float = edge_cot.astype(jnp.float32)
    upstream = active * (cot_float + node_in_grad[:, latent:][edge_dst])
    edge_in_grad, edge_first, edge_second, edge_gain = mlp_backward(
        upstream, inputs, pre_e, hidden_e, normed_e, inv_e, gain_edge, full_edge_in, full_edge_out
    )
    edge_grad = (cot_float + edge_in_grad[:, :latent]).astype(jnp.bfloat16)
    spread = jnp.zeros((padded_side * padded_side, latent), jnp.float32)
    spread = (
        spread.at[source_pad]
        .add(edge_in_grad[:, latent : 2 * latent])
        .at[target_pad]
        .add(edge_in_grad[:, 2 * latent :])
    )
    spread = spread.reshape(padded_side, padded_side, latent)
    outgoing = jnp.stack(
        [
            jnp.stack([spread[1:-1, 0], spread[0, 1:-1]]),
            jnp.stack([spread[-1, 1:-1], spread[1:-1, -1]]),
        ]
    )
    incoming = with_halo(outgoing.astype(jnp.bfloat16), (("dom", 0), ("sub", 1)), 1).astype(
        outgoing.dtype
    )
    inner = spread[1:-1, 1:-1]
    inner = inner.at[0].add(incoming[0, 1]).at[-1].add(incoming[3, 2])
    inner = inner.at[:, 0].add(incoming[2, 0]).at[:, -1].add(incoming[1, 3])
    node_total = node_upstream + node_in_grad[:, :latent]
    node_grad = (node_total.reshape(block_side, block_side, latent) + inner).astype(jnp.bfloat16)
    nodes_all = block_side * block_side * lax.axis_size("dom") * lax.axis_size("sub")
    grad_scale = lax.rsqrt(jnp.float32(nodes_all))
    results = reduce_params(
        (edge_first, edge_second, node_first, node_second), jnp.stack([edge_gain, node_gain]), grad_scale
    )
    return (node_grad, edge_grad) + results


def solution(mesh):
    in_specs = (
        P("dom", "sub", None),
        P(("dom", "sub"), None),
        P(("dom", "sub")),
        P(("dom", "sub")),
        P(("dom", "sub")),
        P("dom", None),
        P("dom", None),
        P("dom", None),
        P("dom", None),
        P(None, "dom"),
        P("dom", "sub", None),
        P(("dom", "sub"), None),
    )
    out_specs = (
        P("dom", "sub", None),
        P(("dom", "sub"), None),
        P("dom", None),
        P("dom", None),
        P("dom", None),
        P("dom", None),
        P(None, "dom"),
    )
    return jax.shard_map(shards, mesh=mesh, in_specs=in_specs, out_specs=out_specs, check_vma=False)
```

```python
import jax
import jax.numpy as jnp
from jax import lax
from jax.sharding import PartitionSpec as P


def with_halo(block, sides, width):
    for axis, dim in sides:
        count = lax.axis_size(axis)
        forward = [(i, i + 1) for i in range(count - 1)]
        backward = [(target, source) for source, target in forward]
        low = lax.ppermute(
            lax.slice_in_dim(block, block.shape[dim] - width, None, axis=dim), axis, forward
        )
        high = lax.ppermute(lax.slice_in_dim(block, 0, width, axis=dim), axis, backward)
        block = jnp.concatenate([low, block, high], axis=dim)
    return block


def layer_norm(raw_out):
    average = jnp.mean(raw_out, axis=-1, keepdims=True)
    centered = raw_out - average
    inv_std = lax.rsqrt(jnp.mean(centered * centered, axis=-1, keepdims=True) + 1e-05)
    return (centered * inv_std, inv_std)


def norm_back(upstream, normed, inv_std):
    return (
        upstream
        - jnp.mean(upstream, axis=-1, keepdims=True)
        - normed * jnp.mean(upstream * normed, axis=-1, keepdims=True)
    ) * inv_std


def mlp_forward(inputs, w_first, w_second, gain_vec):
    pre_act = jnp.dot(inputs, w_first, preferred_element_type=jnp.float32)
    hidden = jnp.maximum(pre_act, 0.0).astype(jnp.bfloat16)
    raw_out = jnp.dot(hidden, w_second, preferred_element_type=jnp.float32)
    normed, inv_std = layer_norm(raw_out)
    return (pre_act, hidden, normed, inv_std, normed * gain_vec)


def mlp_backward(upstream, inputs, pre_act, hidden, normed, inv_std, gain_vec, w_first, w_second):
    gain_part = jnp.sum(upstream * normed, axis=0)
    grad_raw = norm_back(upstream * gain_vec, normed, inv_std).astype(jnp.bfloat16)
    second_part = jnp.dot(hidden.T, grad_raw, preferred_element_type=jnp.float32)
    grad_hidden = jnp.dot(grad_raw, w_second.T, preferred_element_type=jnp.float32)
    grad_pre = jnp.where(pre_act > 0, grad_hidden, 0.0).astype(jnp.bfloat16)
    first_part = jnp.dot(inputs.T, grad_pre, preferred_element_type=jnp.float32)
    grad_inputs = jnp.dot(grad_pre, w_first.T, preferred_element_type=jnp.float32)
    return (grad_inputs, first_part, second_part, gain_part)


def digit_groups(count):
    groups = []
    stride = 1
    rest = count
    while rest > 1:
        radix = 4 if rest % 4 == 0 else (2 if rest % 2 == 0 else rest)
        groups.append((stride, radix))
        stride *= radix
        rest //= radix
    return groups


def shift_digit(value, axis, stride, radix, offset):
    count = lax.axis_size(axis)
    pairs = []
    for i in range(count):
        digit = (i // stride) % radix
        pairs.append((i, i + (((digit + offset) % radix) - digit) * stride))
    return lax.ppermute(value, axis, pairs)


def by_digit(own, received, digit, radix):
    values = [own] + list(received)
    ordered = []
    for position in range(radix):
        source = (digit - position) % radix
        pick = values[0]
        for offset in range(1, radix):
            pick = jnp.where(source == offset, values[offset], pick)
        ordered.append(pick)
    return ordered


def gather_dom(packed):
    index = lax.axis_index("dom")
    block = packed
    for stride, radix in digit_groups(lax.axis_size("dom")):
        digit = (index // stride) % radix
        received = [shift_digit(block, "dom", stride, radix, o) for o in range(1, radix)]
        block = jnp.stack(by_digit(block, received, digit, radix))
    return block.reshape((-1,) + packed.shape)


def reduce_scatter_dom(packed):
    index = lax.axis_index("dom")
    groups = digit_groups(lax.axis_size("dom"))
    block = packed.reshape(tuple(r for _, r in reversed(groups)) + packed.shape[1:])
    for stride, radix in reversed(groups):
        digit = (index // stride) % radix
        parts = [block[p] for p in range(radix)]
        total = parts[0]
        for p in range(1, radix):
            total = jnp.where(digit == p, parts[p], total)
        for offset in range(1, radix):
            target = (digit + offset) % radix
            send = parts[0]
            for p in range(1, radix):
                send = jnp.where(target == p, parts[p], send)
            total = total + shift_digit(send, "dom", stride, radix, offset)
        block = total
    return block


def sum_sub(value):
    index = lax.axis_index("sub")
    total = value
    for stride, radix in digit_groups(lax.axis_size("sub")):
        digit = (index // stride) % radix
        received = [shift_digit(total, "sub", stride, radix, o) for o in range(1, radix)]
        ordered = by_digit(total, received, digit, radix)
        total = ordered[0]
        for item in ordered[1:]:
            total = total + item
    return total


def gather_params(weights, gains):
    latent = weights[0].shape[1]
    gain_row = gains.reshape(1, -1)
    gain_row = jnp.pad(gain_row, ((0, 0), (0, latent - gain_row.shape[1])))
    packed = jnp.concatenate(list(weights) + [gain_row], axis=0)
    full = gather_dom(packed)
    count = full.shape[0]
    outs = []
    start = 0
    for w in weights:
        rows = w.shape[0]
        outs.append(full[:, start : start + rows].reshape(count * rows, latent))
        start += rows
    width = gains.shape[1]
    gain_full = full[:, start, : 2 * width].reshape(count, 2, width)
    gain_full = jnp.transpose(gain_full, (1, 0, 2)).reshape(2, count * width)
    outs.append(gain_full)
    return tuple(outs)


def reduce_params(parts, gain_terms, scale):
    count = lax.axis_size("dom")
    latent = parts[0].shape[1]
    blocks = [p.reshape(count, p.shape[0] // count, latent) for p in parts]
    width = gain_terms.shape[1] // count
    gain_block = jnp.transpose(gain_terms.reshape(2, count, width), (1, 0, 2)).reshape(count, 1, 2 * width)
    gain_block = jnp.pad(gain_block, ((0, 0), (0, 0), (0, latent - 2 * width)))
    packed = jnp.concatenate(blocks + [gain_block], axis=1)
    shard = reduce_scatter_dom(packed)
    shard = sum_sub(shard) * scale
    outs = []
    start = 0
    for b in blocks:
        rows = b.shape[1]
        outs.append(shard[start : start + rows])
        start += rows
    outs.append(shard[start, : 2 * width].reshape(2, width))
    return tuple(outs)


def shards(
    node_feat,
    edge_feat,
    edge_dst,
    edge_dir,
    edge_count,
    w_edge_in,
    w_edge_out,
    w_node_in,
    w_node_out,
    gains,
    node_cot,
    edge_cot,
):
    full_edge_in, full_edge_out, full_node_in, full_node_out, full_gains = gather_params(
        (w_edge_in, w_edge_out, w_node_in, w_node_out), gains
    )
    gain_edge = full_gains[0].astype(jnp.float32)
    gain_node = full_gains[1].astype(jnp.float32)
    block_side = node_feat.shape[0]
    latent = node_feat.shape[2]
    padded_side = block_side + 2
    padded = with_halo(node_feat, (("dom", 0), ("sub", 1)), 1).reshape(
        padded_side * padded_side, latent
    )
    node_row = edge_dst // block_side
    node_col = edge_dst % block_side
    step_row = jnp.where(edge_dir == 0, 1, jnp.where(edge_dir == 1, -1, 0)).astype(jnp.int32)
    step_col = jnp.where(edge_dir == 2, 1, jnp.where(edge_dir == 3, -1, 0)).astype(jnp.int32)
    target_pad = (node_row + 1) * padded_side + node_col + 1
    source_pad = (node_row + 1 + step_row) * padded_side + node_col + 1 + step_col
    active = (jnp.arange(edge_dst.shape[0], dtype=jnp.int32) < edge_count[0]).astype(jnp.float32)[
        :, None
    ]
    inputs = jnp.concatenate([edge_feat, padded[source_pad], padded[target_pad]], axis=1)
    pre_e, hidden_e, normed_e, inv_e, message = mlp_forward(
        inputs, full_edge_in, full_edge_out, gain_edge
    )
    aggregate = jax.ops.segment_sum(
        message * active, edge_dst, num_segments=block_side * block_side
    )
    node_rows = node_feat.reshape(block_side * block_side, latent)
    node_input = jnp.concatenate([node_rows, aggregate.astype(jnp.bfloat16)], axis=1)
    pre_n, hidden_n, normed_n, inv_n, _ = mlp_forward(
        node_input, full_node_in, full_node_out, gain_node
    )
    node_upstream = node_cot.reshape(block_side * block_side, latent).astype(jnp.float32)
    node_in_grad, node_first, node_second, node_gain = mlp_backward(
        node_upstream,
        node_input,
        pre_n,
        hidden_n,
        normed_n,
        inv_n,
        gain_node,
        full_node_in,
        full_node_out,
    )
    cot_float = edge_cot.astype(jnp.float32)
    upstream = active * (cot_float + node_in_grad[:, latent:][edge_dst])
    edge_in_grad, edge_first, edge_second, edge_gain = mlp_backward(
        upstream, inputs, pre_e, hidden_e, normed_e, inv_e, gain_edge, full_edge_in, full_edge_out
    )
    edge_grad = (cot_float + edge_in_grad[:, :latent]).astype(jnp.bfloat16)
    spread = jnp.zeros((padded_side * padded_side, latent), jnp.float32)
    spread = (
        spread.at[source_pad]
        .add(edge_in_grad[:, latent : 2 * latent])
        .at[target_pad]
        .add(edge_in_grad[:, 2 * latent :])
    )
    spread = spread.reshape(padded_side, padded_side, latent)
    outgoing = jnp.stack(
        [
            jnp.stack([spread[1:-1, 0], spread[0, 1:-1]]),
            jnp.stack([spread[-1, 1:-1], spread[1:-1, -1]]),
        ]
    )
    incoming = with_halo(outgoing.astype(jnp.bfloat16), (("dom", 0), ("sub", 1)), 1).astype(
        outgoing.dtype
    )
    inner = spread[1:-1, 1:-1]
    inner = inner.at[0].add(incoming[0, 1]).at[-1].add(incoming[3, 2])
    inner = inner.at[:, 0].add(incoming[2, 0]).at[:, -1].add(incoming[1, 3])
    node_total = node_upstream + node_in_grad[:, :latent]
    node_grad = (node_total.reshape(block_side, block_side, latent) + inner).astype(jnp.bfloat16)
    nodes_all = block_side * block_side * lax.axis_size("dom") * lax.axis_size("sub")
    grad_scale = lax.rsqrt(jnp.float32(nodes_all))
    results = reduce_params(
        (edge_first, edge_second, node_first, node_second), jnp.stack([edge_gain, node_gain]), grad_scale
    )
    return (node_grad, edge_grad) + results


def solution(mesh):
    in_specs = (
        P("dom", "sub", None),
        P(("dom", "sub"), None),
        P(("dom", "sub")),
        P(("dom", "sub")),
        P(("dom", "sub")),
        P("dom", None),
        P("dom", None),
        P("dom", None),
        P("dom", None),
        P(None, "dom"),
        P("dom", "sub", None),
        P(("dom", "sub"), None),
    )
    out_specs = (
        P("dom", "sub", None),
        P(("dom", "sub"), None),
        P("dom", None),
        P("dom", None),
        P("dom", None),
        P("dom", None),
        P(None, "dom"),
    )
    return jax.shard_map(shards, mesh=mesh, in_specs=in_specs, out_specs=out_specs, check_vma=False)
```

```python
import jax
import jax.numpy as jnp
from jax import lax
from jax.sharding import PartitionSpec as P


def with_halo(block, sides, width):
    for axis, dim in sides:
        count = lax.axis_size(axis)
        forward = [(i, i + 1) for i in range(count - 1)]
        backward = [(target, source) for source, target in forward]
        low = lax.ppermute(
            lax.slice_in_dim(block, block.shape[dim] - width, None, axis=dim), axis, forward
        )
        high = lax.ppermute(lax.slice_in_dim(block, 0, width, axis=dim), axis, backward)
        block = jnp.concatenate([low, block, high], axis=dim)
    return block


def layer_norm(raw_out):
    average = jnp.mean(raw_out, axis=-1, keepdims=True)
    centered = raw_out - average
    inv_std = lax.rsqrt(jnp.mean(centered * centered, axis=-1, keepdims=True) + 1e-05)
    return (centered * inv_std, inv_std)


def norm_back(upstream, normed, inv_std):
    return (
        upstream
        - jnp.mean(upstream, axis=-1, keepdims=True)
        - normed * jnp.mean(upstream * normed, axis=-1, keepdims=True)
    ) * inv_std


def mlp_forward(inputs, w_first, w_second, gain_vec):
    pre_act = jnp.dot(inputs, w_first, preferred_element_type=jnp.float32)
    hidden = jnp.maximum(pre_act, 0.0).astype(jnp.bfloat16)
    raw_out = jnp.dot(hidden, w_second, preferred_element_type=jnp.float32)
    normed, inv_std = layer_norm(raw_out)
    return (pre_act, hidden, normed, inv_std, normed * gain_vec)


def mlp_backward(upstream, inputs, pre_act, hidden, normed, inv_std, gain_vec, w_first, w_second):
    gain_part = jnp.sum(upstream * normed, axis=0)
    grad_raw = norm_back(upstream * gain_vec, normed, inv_std).astype(jnp.bfloat16)
    second_part = jnp.dot(hidden.T, grad_raw, preferred_element_type=jnp.float32)
    grad_hidden = jnp.dot(grad_raw, w_second.T, preferred_element_type=jnp.float32)
    grad_pre = jnp.where(pre_act > 0, grad_hidden, 0.0).astype(jnp.bfloat16)
    first_part = jnp.dot(inputs.T, grad_pre, preferred_element_type=jnp.float32)
    grad_inputs = jnp.dot(grad_pre, w_first.T, preferred_element_type=jnp.float32)
    return (grad_inputs, first_part, second_part, gain_part)


def gather_dom(packed):
    count = lax.axis_size("dom")
    spread = jnp.broadcast_to(packed[None], (count,) + packed.shape)
    return lax.all_to_all(spread, "dom", 0, 0, tiled=True)


def reduce_scatter_dom(packed):
    return jnp.sum(lax.all_to_all(packed, "dom", 0, 0, tiled=True), axis=0)


def sum_sub(value):
    count = lax.axis_size("sub")
    flat = value.reshape(count, -1)
    piece = jnp.sum(lax.all_to_all(flat, "sub", 0, 0, tiled=True), axis=0)
    spread = jnp.broadcast_to(piece[None], flat.shape)
    return lax.all_to_all(spread, "sub", 0, 0, tiled=True).reshape(value.shape)


def gather_params(weights, gains):
    latent = weights[0].shape[1]
    gain_row = gains.reshape(1, -1)
    gain_row = jnp.pad(gain_row, ((0, 0), (0, latent - gain_row.shape[1])))
    packed = jnp.concatenate(list(weights) + [gain_row], axis=0)
    full = gather_dom(packed)
    count = full.shape[0]
    outs = []
    start = 0
    for w in weights:
        rows = w.shape[0]
        outs.append(full[:, start : start + rows].reshape(count * rows, latent))
        start += rows
    width = gains.shape[1]
    gain_full = full[:, start, : 2 * width].reshape(count, 2, width)
    gain_full = jnp.transpose(gain_full, (1, 0, 2)).reshape(2, count * width)
    outs.append(gain_full)
    return tuple(outs)


def reduce_params(parts, gain_terms, scale):
    count = lax.axis_size("dom")
    latent = parts[0].shape[1]
    blocks = [p.reshape(count, p.shape[0] // count, latent) for p in parts]
    width = gain_terms.shape[1] // count
    gain_block = jnp.transpose(gain_terms.reshape(2, count, width), (1, 0, 2)).reshape(count, 1, 2 * width)
    gain_block = jnp.pad(gain_block, ((0, 0), (0, 0), (0, latent - 2 * width)))
    packed = jnp.concatenate(blocks + [gain_block], axis=1)
    shard = reduce_scatter_dom(packed)
    shard = sum_sub(shard) * scale
    outs = []
    start = 0
    for b in blocks:
        rows = b.shape[1]
        outs.append(shard[start : start + rows])
        start += rows
    outs.append(shard[start, : 2 * width].reshape(2, width))
    return tuple(outs)


def shards(
    node_feat,
    edge_feat,
    edge_dst,
    edge_dir,
    edge_count,
    w_edge_in,
    w_edge_out,
    w_node_in,
    w_node_out,
    gains,
    node_cot,
    edge_cot,
):
    full_edge_in, full_edge_out, full_node_in, full_node_out, full_gains = gather_params(
        (w_edge_in, w_edge_out, w_node_in, w_node_out), gains
    )
    gain_edge = full_gains[0].astype(jnp.float32)
    gain_node = full_gains[1].astype(jnp.float32)
    block_side = node_feat.shape[0]
    latent = node_feat.shape[2]
    padded_side = block_side + 2
    padded = with_halo(node_feat, (("dom", 0), ("sub", 1)), 1).reshape(
        padded_side * padded_side, latent
    )
    node_row = edge_dst // block_side
    node_col = edge_dst % block_side
    step_row = jnp.where(edge_dir == 0, 1, jnp.where(edge_dir == 1, -1, 0)).astype(jnp.int32)
    step_col = jnp.where(edge_dir == 2, 1, jnp.where(edge_dir == 3, -1, 0)).astype(jnp.int32)
    target_pad = (node_row + 1) * padded_side + node_col + 1
    source_pad = (node_row + 1 + step_row) * padded_side + node_col + 1 + step_col
    active = (jnp.arange(edge_dst.shape[0], dtype=jnp.int32) < edge_count[0]).astype(jnp.float32)[
        :, None
    ]
    inputs = jnp.concatenate([edge_feat, padded[source_pad], padded[target_pad]], axis=1)
    pre_e, hidden_e, normed_e, inv_e, message = mlp_forward(
        inputs, full_edge_in, full_edge_out, gain_edge
    )
    aggregate = jax.ops.segment_sum(
        message * active, edge_dst, num_segments=block_side * block_side
    )
    node_rows = node_feat.reshape(block_side * block_side, latent)
    node_input = jnp.concatenate([node_rows, aggregate.astype(jnp.bfloat16)], axis=1)
    pre_n, hidden_n, normed_n, inv_n, _ = mlp_forward(
        node_input, full_node_in, full_node_out, gain_node
    )
    node_upstream = node_cot.reshape(block_side * block_side, latent).astype(jnp.float32)
    node_in_grad, node_first, node_second, node_gain = mlp_backward(
        node_upstream,
        node_input,
        pre_n,
        hidden_n,
        normed_n,
        inv_n,
        gain_node,
        full_node_in,
        full_node_out,
    )
    cot_float = edge_cot.astype(jnp.float32)
    upstream = active * (cot_float + node_in_grad[:, latent:][edge_dst])
    edge_in_grad, edge_first, edge_second, edge_gain = mlp_backward(
        upstream, inputs, pre_e, hidden_e, normed_e, inv_e, gain_edge, full_edge_in, full_edge_out
    )
    edge_grad = (cot_float + edge_in_grad[:, :latent]).astype(jnp.bfloat16)
    spread = jnp.zeros((padded_side * padded_side, latent), jnp.float32)
    spread = (
        spread.at[source_pad]
        .add(edge_in_grad[:, latent : 2 * latent])
        .at[target_pad]
        .add(edge_in_grad[:, 2 * latent :])
    )
    spread = spread.reshape(padded_side, padded_side, latent)
    outgoing = jnp.stack(
        [
            jnp.stack([spread[1:-1, 0], spread[0, 1:-1]]),
            jnp.stack([spread[-1, 1:-1], spread[1:-1, -1]]),
        ]
    )
    incoming = with_halo(outgoing.astype(jnp.bfloat16), (("dom", 0), ("sub", 1)), 1).astype(
        outgoing.dtype
    )
    inner = spread[1:-1, 1:-1]
    inner = inner.at[0].add(incoming[0, 1]).at[-1].add(incoming[3, 2])
    inner = inner.at[:, 0].add(incoming[2, 0]).at[:, -1].add(incoming[1, 3])
    node_total = node_upstream + node_in_grad[:, :latent]
    node_grad = (node_total.reshape(block_side, block_side, latent) + inner).astype(jnp.bfloat16)
    nodes_all = block_side * block_side * lax.axis_size("dom") * lax.axis_size("sub")
    grad_scale = lax.rsqrt(jnp.float32(nodes_all))
    results = reduce_params(
        (edge_first, edge_second, node_first, node_second), jnp.stack([edge_gain, node_gain]), grad_scale
    )
    return (node_grad, edge_grad) + results


def solution(mesh):
    in_specs = (
        P("dom", "sub", None),
        P(("dom", "sub"), None),
        P(("dom", "sub")),
        P(("dom", "sub")),
        P(("dom", "sub")),
        P("dom", None),
        P("dom", None),
        P("dom", None),
        P("dom", None),
        P(None, "dom"),
        P("dom", "sub", None),
        P(("dom", "sub"), None),
    )
    out_specs = (
        P("dom", "sub", None),
        P(("dom", "sub"), None),
        P("dom", None),
        P("dom", None),
        P("dom", None),
        P("dom", None),
        P(None, "dom"),
    )
    return jax.shard_map(shards, mesh=mesh, in_specs=in_specs, out_specs=out_specs, check_vma=False)
```

```python
import jax
import jax.numpy as jnp
from jax import lax
from jax.sharding import PartitionSpec as P


def with_halo(block, sides, width):
    for axis, dim in sides:
        count = lax.axis_size(axis)
        forward = [(i, i + 1) for i in range(count - 1)]
        backward = [(target, source) for source, target in forward]
        low = lax.ppermute(
            lax.slice_in_dim(block, block.shape[dim] - width, None, axis=dim), axis, forward
        )
        high = lax.ppermute(lax.slice_in_dim(block, 0, width, axis=dim), axis, backward)
        block = jnp.concatenate([low, block, high], axis=dim)
    return block


def layer_norm(raw_out):
    average = jnp.mean(raw_out, axis=-1, keepdims=True)
    centered = raw_out - average
    inv_std = lax.rsqrt(jnp.mean(centered * centered, axis=-1, keepdims=True) + 1e-05)
    return (centered * inv_std, inv_std)


def norm_back(upstream, normed, inv_std):
    return (
        upstream
        - jnp.mean(upstream, axis=-1, keepdims=True)
        - normed * jnp.mean(upstream * normed, axis=-1, keepdims=True)
    ) * inv_std


def mlp_forward(inputs, w_first, w_second, gain_vec):
    pre_act = jnp.dot(inputs, w_first, preferred_element_type=jnp.float32)
    hidden = jnp.maximum(pre_act, 0.0).astype(jnp.bfloat16)
    raw_out = jnp.dot(hidden, w_second, preferred_element_type=jnp.float32)
    normed, inv_std = layer_norm(raw_out)
    return (pre_act, hidden, normed, inv_std, normed * gain_vec)


def mlp_backward(upstream, inputs, pre_act, hidden, normed, inv_std, gain_vec, w_first, w_second):
    gain_part = jnp.sum(upstream * normed, axis=0)
    grad_raw = norm_back(upstream * gain_vec, normed, inv_std).astype(jnp.bfloat16)
    second_part = jnp.dot(hidden.T, grad_raw, preferred_element_type=jnp.float32)
    grad_hidden = jnp.dot(grad_raw, w_second.T, preferred_element_type=jnp.float32)
    grad_pre = jnp.where(pre_act > 0, grad_hidden, 0.0).astype(jnp.bfloat16)
    first_part = jnp.dot(inputs.T, grad_pre, preferred_element_type=jnp.float32)
    grad_inputs = jnp.dot(grad_pre, w_first.T, preferred_element_type=jnp.float32)
    return (grad_inputs, first_part, second_part, gain_part)


def gather_dom(packed):
    count = lax.axis_size("dom")
    spread = jnp.broadcast_to(packed[None], (count,) + packed.shape)
    return lax.all_to_all(spread, "dom", 0, 0, tiled=True)


def reduce_scatter_dom(packed):
    return jnp.sum(lax.all_to_all(packed, "dom", 0, 0, tiled=True), axis=0)


def sum_sub(value):
    count = lax.axis_size("sub")
    flat = value.reshape(count, -1)
    piece = jnp.sum(lax.all_to_all(flat, "sub", 0, 0, tiled=True), axis=0)
    spread = jnp.broadcast_to(piece[None], flat.shape)
    return lax.all_to_all(spread, "sub", 0, 0, tiled=True).reshape(value.shape)


def gather_params(weights, gains):
    latent = weights[0].shape[1]
    gain_row = gains.reshape(1, -1)
    gain_row = jnp.pad(gain_row, ((0, 0), (0, latent - gain_row.shape[1])))
    packed = jnp.concatenate(list(weights) + [gain_row], axis=0)
    full = gather_dom(packed)
    count = full.shape[0]
    outs = []
    start = 0
    for w in weights:
        rows = w.shape[0]
        outs.append(full[:, start : start + rows].reshape(count * rows, latent))
        start += rows
    width = gains.shape[1]
    gain_full = full[:, start, : 2 * width].reshape(count, 2, width)
    gain_full = jnp.transpose(gain_full, (1, 0, 2)).reshape(2, count * width)
    outs.append(gain_full)
    return tuple(outs)


def reduce_params(parts, gain_terms, scale):
    count = lax.axis_size("dom")
    latent = parts[0].shape[1]
    blocks = [p.reshape(count, p.shape[0] // count, latent) for p in parts]
    width = gain_terms.shape[1] // count
    gain_block = jnp.transpose(gain_terms.reshape(2, count, width), (1, 0, 2)).reshape(count, 1, 2 * width)
    gain_block = jnp.pad(gain_block, ((0, 0), (0, 0), (0, latent - 2 * width)))
    packed = jnp.concatenate(blocks + [gain_block], axis=1)
    shard = reduce_scatter_dom(packed)
    shard = sum_sub(shard) * scale
    outs = []
    start = 0
    for b in blocks:
        rows = b.shape[1]
        outs.append(shard[start : start + rows])
        start += rows
    outs.append(shard[start, : 2 * width].reshape(2, width))
    return tuple(outs)


def one_hot(index, count):
    return (index[:, None] == jnp.arange(count, dtype=index.dtype)[None, :]).astype(jnp.bfloat16)


def select_rows(pick, table):
    if table.dtype == jnp.bfloat16:
        return jnp.dot(pick, table, preferred_element_type=jnp.float32).astype(jnp.bfloat16)
    return jnp.dot(
        pick.astype(jnp.float32), table, precision=lax.Precision.HIGHEST, preferred_element_type=jnp.float32
    )


def sum_rows(pick, values):
    return lax.dot_general(
        pick.astype(jnp.float32),
        values,
        (((0,), (0,)), ((), ())),
        precision=lax.Precision.HIGHEST,
        preferred_element_type=jnp.float32,
    )


def shards(
    node_feat,
    edge_feat,
    edge_dst,
    edge_dir,
    edge_count,
    w_edge_in,
    w_edge_out,
    w_node_in,
    w_node_out,
    gains,
    node_cot,
    edge_cot,
):
    full_edge_in, full_edge_out, full_node_in, full_node_out, full_gains = gather_params(
        (w_edge_in, w_edge_out, w_node_in, w_node_out), gains
    )
    gain_edge = full_gains[0].astype(jnp.float32)
    gain_node = full_gains[1].astype(jnp.float32)
    block_side = node_feat.shape[0]
    latent = node_feat.shape[2]
    padded_side = block_side + 2
    padded = with_halo(node_feat, (("dom", 0), ("sub", 1)), 1).reshape(
        padded_side * padded_side, latent
    )
    node_row = edge_dst // block_side
    node_col = edge_dst % block_side
    step_row = jnp.where(edge_dir == 0, 1, jnp.where(edge_dir == 1, -1, 0)).astype(jnp.int32)
    step_col = jnp.where(edge_dir == 2, 1, jnp.where(edge_dir == 3, -1, 0)).astype(jnp.int32)
    target_pad = (node_row + 1) * padded_side + node_col + 1
    source_pad = (node_row + 1 + step_row) * padded_side + node_col + 1 + step_col
    active = (jnp.arange(edge_dst.shape[0], dtype=jnp.int32) < edge_count[0]).astype(jnp.float32)[
        :, None
    ]
    padded_count = padded_side * padded_side
    pick_source = one_hot(source_pad, padded_count)
    pick_target = one_hot(target_pad, padded_count)
    pick_local = one_hot(edge_dst, block_side * block_side)
    inputs = jnp.concatenate(
        [edge_feat, select_rows(pick_source, padded), select_rows(pick_target, padded)], axis=1
    )
    pre_e, hidden_e, normed_e, inv_e, message = mlp_forward(
        inputs, full_edge_in, full_edge_out, gain_edge
    )
    aggregate = sum_rows(pick_local, message * active)
    node_rows = node_feat.reshape(block_side * block_side, latent)
    node_input = jnp.concatenate([node_rows, aggregate.astype(jnp.bfloat16)], axis=1)
    pre_n, hidden_n, normed_n, inv_n, _ = mlp_forward(
        node_input, full_node_in, full_node_out, gain_node
    )
    node_upstream = node_cot.reshape(block_side * block_side, latent).astype(jnp.float32)
    node_in_grad, node_first, node_second, node_gain = mlp_backward(
        node_upstream,
        node_input,
        pre_n,
        hidden_n,
        normed_n,
        inv_n,
        gain_node,
        full_node_in,
        full_node_out,
    )
    cot_float = edge_cot.astype(jnp.float32)
    upstream = active * (cot_float + select_rows(pick_local, node_in_grad[:, latent:]))
    edge_in_grad, edge_first, edge_second, edge_gain = mlp_backward(
        upstream, inputs, pre_e, hidden_e, normed_e, inv_e, gain_edge, full_edge_in, full_edge_out
    )
    edge_grad = (cot_float + edge_in_grad[:, :latent]).astype(jnp.bfloat16)
    spread = sum_rows(
        jnp.concatenate([pick_source, pick_target], axis=0),
        jnp.concatenate([edge_in_grad[:, latent : 2 * latent], edge_in_grad[:, 2 * latent :]], axis=0),
    )
    spread = spread.reshape(padded_side, padded_side, latent)
    outgoing = jnp.stack(
        [
            jnp.stack([spread[1:-1, 0], spread[0, 1:-1]]),
            jnp.stack([spread[-1, 1:-1], spread[1:-1, -1]]),
        ]
    )
    incoming = with_halo(outgoing.astype(jnp.bfloat16), (("dom", 0), ("sub", 1)), 1).astype(
        outgoing.dtype
    )
    inner = spread[1:-1, 1:-1]
    inner = inner.at[0].add(incoming[0, 1]).at[-1].add(incoming[3, 2])
    inner = inner.at[:, 0].add(incoming[2, 0]).at[:, -1].add(incoming[1, 3])
    node_total = node_upstream + node_in_grad[:, :latent]
    node_grad = (node_total.reshape(block_side, block_side, latent) + inner).astype(jnp.bfloat16)
    nodes_all = block_side * block_side * lax.axis_size("dom") * lax.axis_size("sub")
    grad_scale = lax.rsqrt(jnp.float32(nodes_all))
    results = reduce_params(
        (edge_first, edge_second, node_first, node_second), jnp.stack([edge_gain, node_gain]), grad_scale
    )
    return (node_grad, edge_grad) + results


def solution(mesh):
    in_specs = (
        P("dom", "sub", None),
        P(("dom", "sub"), None),
        P(("dom", "sub")),
        P(("dom", "sub")),
        P(("dom", "sub")),
        P("dom", None),
        P("dom", None),
        P("dom", None),
        P("dom", None),
        P(None, "dom"),
        P("dom", "sub", None),
        P(("dom", "sub"), None),
    )
    out_specs = (
        P("dom", "sub", None),
        P(("dom", "sub"), None),
        P("dom", None),
        P("dom", None),
        P("dom", None),
        P("dom", None),
        P(None, "dom"),
    )
    return jax.shard_map(shards, mesh=mesh, in_specs=in_specs, out_specs=out_specs, check_vma=False)
```

```python
import jax
import jax.numpy as jnp
from jax import lax
from jax.sharding import PartitionSpec as P


def with_halo(block, sides, width):
    for axis, dim in sides:
        count = lax.axis_size(axis)
        forward = [(i, i + 1) for i in range(count - 1)]
        backward = [(target, source) for source, target in forward]
        low = lax.ppermute(
            lax.slice_in_dim(block, block.shape[dim] - width, None, axis=dim), axis, forward
        )
        high = lax.ppermute(lax.slice_in_dim(block, 0, width, axis=dim), axis, backward)
        block = jnp.concatenate([low, block, high], axis=dim)
    return block


def layer_norm(raw_out):
    average = jnp.mean(raw_out, axis=-1, keepdims=True)
    centered = raw_out - average
    inv_std = lax.rsqrt(jnp.mean(centered * centered, axis=-1, keepdims=True) + 1e-05)
    return (centered * inv_std, inv_std)


def norm_back(upstream, normed, inv_std):
    return (
        upstream
        - jnp.mean(upstream, axis=-1, keepdims=True)
        - normed * jnp.mean(upstream * normed, axis=-1, keepdims=True)
    ) * inv_std


def mlp_forward(inputs, w_first, w_second, gain_vec):
    pre_act = jnp.dot(inputs, w_first, preferred_element_type=jnp.float32)
    hidden = jnp.maximum(pre_act, 0.0).astype(jnp.bfloat16)
    raw_out = jnp.dot(hidden, w_second, preferred_element_type=jnp.float32)
    normed, inv_std = layer_norm(raw_out)
    return (pre_act, hidden, normed, inv_std, normed * gain_vec)


def mlp_backward(upstream, inputs, pre_act, hidden, normed, inv_std, gain_vec, w_first, w_second):
    gain_part = jnp.sum(upstream * normed, axis=0)
    grad_raw = norm_back(upstream * gain_vec, normed, inv_std).astype(jnp.bfloat16)
    second_part = jnp.dot(hidden.T, grad_raw, preferred_element_type=jnp.float32)
    grad_hidden = jnp.dot(grad_raw, w_second.T, preferred_element_type=jnp.float32)
    grad_pre = jnp.where(pre_act > 0, grad_hidden, 0.0).astype(jnp.bfloat16)
    first_part = jnp.dot(inputs.T, grad_pre, preferred_element_type=jnp.float32)
    grad_inputs = jnp.dot(grad_pre, w_first.T, preferred_element_type=jnp.float32)
    return (grad_inputs, first_part, second_part, gain_part)


def gather_dom(packed):
    count = lax.axis_size("dom")
    spread = jnp.broadcast_to(packed[None], (count,) + packed.shape)
    return lax.all_to_all(spread, "dom", 0, 0, tiled=True)


def reduce_scatter_dom(packed):
    return jnp.sum(lax.all_to_all(packed, "dom", 0, 0, tiled=True), axis=0)


def sum_sub(value):
    count = lax.axis_size("sub")
    spread = jnp.broadcast_to(value[None], (count,) + value.shape)
    return jnp.sum(lax.all_to_all(spread, "sub", 0, 0, tiled=True), axis=0)


def gather_params(weights, gains):
    latent = weights[0].shape[1]
    gain_row = gains.reshape(1, -1)
    gain_row = jnp.pad(gain_row, ((0, 0), (0, latent - gain_row.shape[1])))
    packed = jnp.concatenate(list(weights) + [gain_row], axis=0)
    full = gather_dom(packed)
    count = full.shape[0]
    outs = []
    start = 0
    for w in weights:
        rows = w.shape[0]
        outs.append(full[:, start : start + rows].reshape(count * rows, latent))
        start += rows
    width = gains.shape[1]
    gain_full = full[:, start, : 2 * width].reshape(count, 2, width)
    gain_full = jnp.transpose(gain_full, (1, 0, 2)).reshape(2, count * width)
    outs.append(gain_full)
    return tuple(outs)


def reduce_params(parts, gain_terms, scale):
    count = lax.axis_size("dom")
    latent = parts[0].shape[1]
    blocks = [p.reshape(count, p.shape[0] // count, latent) for p in parts]
    width = gain_terms.shape[1] // count
    gain_block = jnp.transpose(gain_terms.reshape(2, count, width), (1, 0, 2)).reshape(count, 1, 2 * width)
    gain_block = jnp.pad(gain_block, ((0, 0), (0, 0), (0, latent - 2 * width)))
    packed = jnp.concatenate(blocks + [gain_block], axis=1)
    shard = reduce_scatter_dom(packed)
    shard = sum_sub(shard) * scale
    outs = []
    start = 0
    for b in blocks:
        rows = b.shape[1]
        outs.append(shard[start : start + rows])
        start += rows
    outs.append(shard[start, : 2 * width].reshape(2, width))
    return tuple(outs)


def one_hot(index, count):
    return (index[:, None] == jnp.arange(count, dtype=index.dtype)[None, :]).astype(jnp.bfloat16)


def select_rows(pick, table):
    if table.dtype == jnp.bfloat16:
        return jnp.dot(pick, table, preferred_element_type=jnp.float32).astype(jnp.bfloat16)
    return jnp.dot(
        pick.astype(jnp.float32), table, precision=lax.Precision.HIGHEST, preferred_element_type=jnp.float32
    )


def sum_rows(pick, values):
    return lax.dot_general(
        pick.astype(jnp.float32),
        values,
        (((0,), (0,)), ((), ())),
        precision=lax.Precision.HIGHEST,
        preferred_element_type=jnp.float32,
    )


def shards(
    node_feat,
    edge_feat,
    edge_dst,
    edge_dir,
    edge_count,
    w_edge_in,
    w_edge_out,
    w_node_in,
    w_node_out,
    gains,
    node_cot,
    edge_cot,
):
    full_edge_in, full_edge_out, full_node_in, full_node_out, full_gains = gather_params(
        (w_edge_in, w_edge_out, w_node_in, w_node_out), gains
    )
    gain_edge = full_gains[0].astype(jnp.float32)
    gain_node = full_gains[1].astype(jnp.float32)
    block_side = node_feat.shape[0]
    latent = node_feat.shape[2]
    padded_side = block_side + 2
    padded = with_halo(node_feat, (("dom", 0), ("sub", 1)), 1).reshape(
        padded_side * padded_side, latent
    )
    node_row = edge_dst // block_side
    node_col = edge_dst % block_side
    step_row = jnp.where(edge_dir == 0, 1, jnp.where(edge_dir == 1, -1, 0)).astype(jnp.int32)
    step_col = jnp.where(edge_dir == 2, 1, jnp.where(edge_dir == 3, -1, 0)).astype(jnp.int32)
    target_pad = (node_row + 1) * padded_side + node_col + 1
    source_pad = (node_row + 1 + step_row) * padded_side + node_col + 1 + step_col
    active = (jnp.arange(edge_dst.shape[0], dtype=jnp.int32) < edge_count[0]).astype(jnp.float32)[
        :, None
    ]
    padded_count = padded_side * padded_side
    pick_source = one_hot(source_pad, padded_count)
    pick_target = one_hot(target_pad, padded_count)
    pick_local = one_hot(edge_dst, block_side * block_side)
    inputs = jnp.concatenate(
        [edge_feat, select_rows(pick_source, padded), select_rows(pick_target, padded)], axis=1
    )
    pre_e, hidden_e, normed_e, inv_e, message = mlp_forward(
        inputs, full_edge_in, full_edge_out, gain_edge
    )
    aggregate = sum_rows(pick_local, message * active)
    node_rows = node_feat.reshape(block_side * block_side, latent)
    node_input = jnp.concatenate([node_rows, aggregate.astype(jnp.bfloat16)], axis=1)
    pre_n, hidden_n, normed_n, inv_n, _ = mlp_forward(
        node_input, full_node_in, full_node_out, gain_node
    )
    node_upstream = node_cot.reshape(block_side * block_side, latent).astype(jnp.float32)
    node_in_grad, node_first, node_second, node_gain = mlp_backward(
        node_upstream,
        node_input,
        pre_n,
        hidden_n,
        normed_n,
        inv_n,
        gain_node,
        full_node_in,
        full_node_out,
    )
    cot_float = edge_cot.astype(jnp.float32)
    upstream = active * (cot_float + select_rows(pick_local, node_in_grad[:, latent:]))
    edge_in_grad, edge_first, edge_second, edge_gain = mlp_backward(
        upstream, inputs, pre_e, hidden_e, normed_e, inv_e, gain_edge, full_edge_in, full_edge_out
    )
    edge_grad = (cot_float + edge_in_grad[:, :latent]).astype(jnp.bfloat16)
    spread = sum_rows(
        jnp.concatenate([pick_source, pick_target], axis=0),
        jnp.concatenate([edge_in_grad[:, latent : 2 * latent], edge_in_grad[:, 2 * latent :]], axis=0),
    )
    spread = spread.reshape(padded_side, padded_side, latent)
    outgoing = jnp.stack(
        [
            jnp.stack([spread[1:-1, 0], spread[0, 1:-1]]),
            jnp.stack([spread[-1, 1:-1], spread[1:-1, -1]]),
        ]
    )
    incoming = with_halo(outgoing.astype(jnp.bfloat16), (("dom", 0), ("sub", 1)), 1).astype(
        outgoing.dtype
    )
    inner = spread[1:-1, 1:-1]
    inner = inner.at[0].add(incoming[0, 1]).at[-1].add(incoming[3, 2])
    inner = inner.at[:, 0].add(incoming[2, 0]).at[:, -1].add(incoming[1, 3])
    node_total = node_upstream + node_in_grad[:, :latent]
    node_grad = (node_total.reshape(block_side, block_side, latent) + inner).astype(jnp.bfloat16)
    nodes_all = block_side * block_side * lax.axis_size("dom") * lax.axis_size("sub")
    grad_scale = lax.rsqrt(jnp.float32(nodes_all))
    results = reduce_params(
        (edge_first, edge_second, node_first, node_second), jnp.stack([edge_gain, node_gain]), grad_scale
    )
    return (node_grad, edge_grad) + results


def solution(mesh):
    in_specs = (
        P("dom", "sub", None),
        P(("dom", "sub"), None),
        P(("dom", "sub")),
        P(("dom", "sub")),
        P(("dom", "sub")),
        P("dom", None),
        P("dom", None),
        P("dom", None),
        P("dom", None),
        P(None, "dom"),
        P("dom", "sub", None),
        P(("dom", "sub"), None),
    )
    out_specs = (
        P("dom", "sub", None),
        P(("dom", "sub"), None),
        P("dom", None),
        P("dom", None),
        P("dom", None),
        P("dom", None),
        P(None, "dom"),
    )
    return jax.shard_map(shards, mesh=mesh, in_specs=in_specs, out_specs=out_specs, check_vma=False)
```

```python
import jax
import jax.numpy as jnp
from jax import lax
from jax.sharding import PartitionSpec as P


def with_halo(block, sides, width):
    for axis, dim in sides:
        count = lax.axis_size(axis)
        forward = [(i, i + 1) for i in range(count - 1)]
        backward = [(target, source) for source, target in forward]
        low = lax.ppermute(
            lax.slice_in_dim(block, block.shape[dim] - width, None, axis=dim), axis, forward
        )
        high = lax.ppermute(lax.slice_in_dim(block, 0, width, axis=dim), axis, backward)
        block = jnp.concatenate([low, block, high], axis=dim)
    return block


def layer_norm(raw_out):
    average = jnp.mean(raw_out, axis=-1, keepdims=True)
    centered = raw_out - average
    inv_std = lax.rsqrt(jnp.mean(centered * centered, axis=-1, keepdims=True) + 1e-05)
    return (centered * inv_std, inv_std)


def norm_back(upstream, normed, inv_std):
    return (
        upstream
        - jnp.mean(upstream, axis=-1, keepdims=True)
        - normed * jnp.mean(upstream * normed, axis=-1, keepdims=True)
    ) * inv_std


def mlp_forward(inputs, w_first, w_second, gain_vec):
    pre_act = jnp.dot(inputs, w_first, preferred_element_type=jnp.float32)
    hidden = jnp.maximum(pre_act, 0.0).astype(jnp.bfloat16)
    raw_out = jnp.dot(hidden, w_second, preferred_element_type=jnp.float32)
    normed, inv_std = layer_norm(raw_out)
    return (pre_act, hidden, normed, inv_std, normed * gain_vec)


def mlp_backward(upstream, inputs, pre_act, hidden, normed, inv_std, gain_vec, w_first, w_second):
    gain_part = jnp.sum(upstream * normed, axis=0)
    grad_raw = norm_back(upstream * gain_vec, normed, inv_std).astype(jnp.bfloat16)
    second_part = jnp.dot(hidden.T, grad_raw, preferred_element_type=jnp.float32)
    grad_hidden = jnp.dot(grad_raw, w_second.T, preferred_element_type=jnp.float32)
    grad_pre = jnp.where(pre_act > 0, grad_hidden, 0.0).astype(jnp.bfloat16)
    first_part = jnp.dot(inputs.T, grad_pre, preferred_element_type=jnp.float32)
    grad_inputs = jnp.dot(grad_pre, w_first.T, preferred_element_type=jnp.float32)
    return (grad_inputs, first_part, second_part, gain_part)


def exchange(value, axis, mask):
    count = lax.axis_size(axis)
    return lax.ppermute(value, axis, [(i, i ^ mask) for i in range(count)])


def bit_masks(count):
    masks = []
    mask = 1
    while mask < count:
        masks.append(mask)
        mask *= 2
    return masks


def gather_dom(packed):
    count = lax.axis_size("dom")
    spread = jnp.broadcast_to(packed[None], (count,) + packed.shape)
    return lax.all_to_all(spread, "dom", 0, 0, tiled=True)


def reduce_scatter_dom(packed):
    return jnp.sum(lax.all_to_all(packed, "dom", 0, 0, tiled=True), axis=0)


def sum_sub(value):
    count = lax.axis_size("sub")
    index = lax.axis_index("sub")
    total = value
    mask = 1
    while count % (2 * mask) == 0:
        total = total + exchange(total, "sub", mask)
        mask *= 2
    rest = count // mask
    if rest > 1:
        member = index // mask
        shifted = [total] + [
            lax.ppermute(total, "sub", [(i, (i + k * mask) % count) for i in range(count)])
            for k in range(1, rest)
        ]
        stacked = jnp.stack(shifted)
        ordered = lax.dynamic_index_in_dim(stacked, member % rest, keepdims=False)
        for source in range(1, rest):
            pick = (member - source) % rest
            ordered = ordered + lax.dynamic_index_in_dim(stacked, pick, keepdims=False)
        total = ordered
    return total


def gather_params(weights, gains):
    latent = weights[0].shape[1]
    gain_row = gains.reshape(1, -1)
    gain_row = jnp.pad(gain_row, ((0, 0), (0, latent - gain_row.shape[1])))
    packed = jnp.concatenate(list(weights) + [gain_row], axis=0)
    full = gather_dom(packed)
    count = full.shape[0]
    outs = []
    start = 0
    for w in weights:
        rows = w.shape[0]
        outs.append(full[:, start : start + rows].reshape(count * rows, latent))
        start += rows
    width = gains.shape[1]
    gain_full = full[:, start, : 2 * width].reshape(count, 2, width)
    gain_full = jnp.transpose(gain_full, (1, 0, 2)).reshape(2, count * width)
    outs.append(gain_full)
    return tuple(outs)


def reduce_params(parts, gain_terms, scale):
    count = lax.axis_size("dom")
    latent = parts[0].shape[1]
    blocks = [p.reshape(count, p.shape[0] // count, latent) for p in parts]
    width = gain_terms.shape[1] // count
    gain_block = jnp.transpose(gain_terms.reshape(2, count, width), (1, 0, 2)).reshape(count, 1, 2 * width)
    gain_block = jnp.pad(gain_block, ((0, 0), (0, 0), (0, latent - 2 * width)))
    packed = jnp.concatenate(blocks + [gain_block], axis=1)
    shard = reduce_scatter_dom(packed)
    shard = sum_sub(shard) * scale
    outs = []
    start = 0
    for b in blocks:
        rows = b.shape[1]
        outs.append(shard[start : start + rows])
        start += rows
    outs.append(shard[start, : 2 * width].reshape(2, width))
    return tuple(outs)


def one_hot(index, count):
    return (index[:, None] == jnp.arange(count, dtype=index.dtype)[None, :]).astype(jnp.bfloat16)


def select_rows(pick, table):
    if table.dtype == jnp.bfloat16:
        return jnp.dot(pick, table, preferred_element_type=jnp.float32).astype(jnp.bfloat16)
    return jnp.dot(
        pick.astype(jnp.float32), table, precision=lax.Precision.HIGHEST, preferred_element_type=jnp.float32
    )


def sum_rows(pick, values):
    return lax.dot_general(
        pick.astype(jnp.float32),
        values,
        (((0,), (0,)), ((), ())),
        precision=lax.Precision.HIGHEST,
        preferred_element_type=jnp.float32,
    )


def shards(
    node_feat,
    edge_feat,
    edge_dst,
    edge_dir,
    edge_count,
    w_edge_in,
    w_edge_out,
    w_node_in,
    w_node_out,
    gains,
    node_cot,
    edge_cot,
):
    full_edge_in, full_edge_out, full_node_in, full_node_out, full_gains = gather_params(
        (w_edge_in, w_edge_out, w_node_in, w_node_out), gains
    )
    gain_edge = full_gains[0].astype(jnp.float32)
    gain_node = full_gains[1].astype(jnp.float32)
    block_side = node_feat.shape[0]
    latent = node_feat.shape[2]
    padded_side = block_side + 2
    padded = with_halo(node_feat, (("dom", 0), ("sub", 1)), 1).reshape(
        padded_side * padded_side, latent
    )
    node_row = edge_dst // block_side
    node_col = edge_dst % block_side
    step_row = jnp.where(edge_dir == 0, 1, jnp.where(edge_dir == 1, -1, 0)).astype(jnp.int32)
    step_col = jnp.where(edge_dir == 2, 1, jnp.where(edge_dir == 3, -1, 0)).astype(jnp.int32)
    target_pad = (node_row + 1) * padded_side + node_col + 1
    source_pad = (node_row + 1 + step_row) * padded_side + node_col + 1 + step_col
    active = (jnp.arange(edge_dst.shape[0], dtype=jnp.int32) < edge_count[0]).astype(jnp.float32)[
        :, None
    ]
    padded_count = padded_side * padded_side
    pick_source = one_hot(source_pad, padded_count)
    pick_target = one_hot(target_pad, padded_count)
    pick_local = one_hot(edge_dst, block_side * block_side)
    inputs = jnp.concatenate(
        [edge_feat, select_rows(pick_source, padded), select_rows(pick_target, padded)], axis=1
    )
    pre_e, hidden_e, normed_e, inv_e, message = mlp_forward(
        inputs, full_edge_in, full_edge_out, gain_edge
    )
    aggregate = sum_rows(pick_local, message * active)
    node_rows = node_feat.reshape(block_side * block_side, latent)
    node_input = jnp.concatenate([node_rows, aggregate.astype(jnp.bfloat16)], axis=1)
    pre_n, hidden_n, normed_n, inv_n, _ = mlp_forward(
        node_input, full_node_in, full_node_out, gain_node
    )
    node_upstream = node_cot.reshape(block_side * block_side, latent).astype(jnp.float32)
    node_in_grad, node_first, node_second, node_gain = mlp_backward(
        node_upstream,
        node_input,
        pre_n,
        hidden_n,
        normed_n,
        inv_n,
        gain_node,
        full_node_in,
        full_node_out,
    )
    cot_float = edge_cot.astype(jnp.float32)
    upstream = active * (cot_float + select_rows(pick_local, node_in_grad[:, latent:]))
    edge_in_grad, edge_first, edge_second, edge_gain = mlp_backward(
        upstream, inputs, pre_e, hidden_e, normed_e, inv_e, gain_edge, full_edge_in, full_edge_out
    )
    edge_grad = (cot_float + edge_in_grad[:, :latent]).astype(jnp.bfloat16)
    spread = sum_rows(
        jnp.concatenate([pick_source, pick_target], axis=0),
        jnp.concatenate([edge_in_grad[:, latent : 2 * latent], edge_in_grad[:, 2 * latent :]], axis=0),
    )
    spread = spread.reshape(padded_side, padded_side, latent)
    outgoing = jnp.stack(
        [
            jnp.stack([spread[1:-1, 0], spread[0, 1:-1]]),
            jnp.stack([spread[-1, 1:-1], spread[1:-1, -1]]),
        ]
    )
    incoming = with_halo(outgoing.astype(jnp.bfloat16), (("dom", 0), ("sub", 1)), 1).astype(
        outgoing.dtype
    )
    inner = spread[1:-1, 1:-1]
    inner = inner.at[0].add(incoming[0, 1]).at[-1].add(incoming[3, 2])
    inner = inner.at[:, 0].add(incoming[2, 0]).at[:, -1].add(incoming[1, 3])
    node_total = node_upstream + node_in_grad[:, :latent]
    node_grad = (node_total.reshape(block_side, block_side, latent) + inner).astype(jnp.bfloat16)
    nodes_all = block_side * block_side * lax.axis_size("dom") * lax.axis_size("sub")
    grad_scale = lax.rsqrt(jnp.float32(nodes_all))
    results = reduce_params(
        (edge_first, edge_second, node_first, node_second), jnp.stack([edge_gain, node_gain]), grad_scale
    )
    return (node_grad, edge_grad) + results


def solution(mesh):
    in_specs = (
        P("dom", "sub", None),
        P(("dom", "sub"), None),
        P(("dom", "sub")),
        P(("dom", "sub")),
        P(("dom", "sub")),
        P("dom", None),
        P("dom", None),
        P("dom", None),
        P("dom", None),
        P(None, "dom"),
        P("dom", "sub", None),
        P(("dom", "sub"), None),
    )
    out_specs = (
        P("dom", "sub", None),
        P(("dom", "sub"), None),
        P("dom", None),
        P("dom", None),
        P("dom", None),
        P("dom", None),
        P(None, "dom"),
    )
    return jax.shard_map(shards, mesh=mesh, in_specs=in_specs, out_specs=out_specs, check_vma=False)
```

```python
import jax
import jax.numpy as jnp
from jax import lax
from jax.sharding import PartitionSpec as P


def with_halo(block, sides, width):
    for axis, dim in sides:
        count = axis_count(axis)
        forward = [(i, i + 1) for i in range(count - 1)]
        backward = [(target, source) for source, target in forward]
        low = lax.ppermute(
            lax.slice_in_dim(block, block.shape[dim] - width, None, axis=dim), axis, forward
        )
        high = lax.ppermute(lax.slice_in_dim(block, 0, width, axis=dim), axis, backward)
        block = jnp.concatenate([low, block, high], axis=dim)
    return block


def layer_norm(raw_out):
    average = jnp.mean(raw_out, axis=-1, keepdims=True)
    centered = raw_out - average
    inv_std = lax.rsqrt(jnp.mean(centered * centered, axis=-1, keepdims=True) + 1e-05)
    return (centered * inv_std, inv_std)


def norm_back(upstream, normed, inv_std):
    return (
        upstream
        - jnp.mean(upstream, axis=-1, keepdims=True)
        - normed * jnp.mean(upstream * normed, axis=-1, keepdims=True)
    ) * inv_std


def mlp_forward(inputs, w_first, w_second, gain_vec):
    pre_act = jnp.dot(inputs, w_first, preferred_element_type=jnp.float32)
    hidden = jnp.maximum(pre_act, 0.0).astype(jnp.bfloat16)
    raw_out = jnp.dot(hidden, w_second, preferred_element_type=jnp.float32)
    normed, inv_std = layer_norm(raw_out)
    return (pre_act, hidden, normed, inv_std, normed * gain_vec)


def mlp_backward(upstream, inputs, pre_act, hidden, normed, inv_std, gain_vec, w_first, w_second):
    gain_part = jnp.sum(upstream * normed, axis=0)
    grad_raw = norm_back(upstream * gain_vec, normed, inv_std).astype(jnp.bfloat16)
    second_part = jnp.dot(hidden.T, grad_raw, preferred_element_type=jnp.float32)
    grad_hidden = jnp.dot(grad_raw, w_second.T, preferred_element_type=jnp.float32)
    grad_pre = jnp.where(pre_act > 0, grad_hidden, 0.0).astype(jnp.bfloat16)
    first_part = jnp.dot(inputs.T, grad_pre, preferred_element_type=jnp.float32)
    grad_inputs = jnp.dot(grad_pre, w_first.T, preferred_element_type=jnp.float32)
    return (grad_inputs, first_part, second_part, gain_part)


SUB = ("sub_hi", "sub_lo")


def axis_count(axis):
    if isinstance(axis, tuple):
        total = 1
        for name in axis:
            total *= lax.axis_size(name)
        return total
    return lax.axis_size(axis)


def exchange(value, axis, mask):
    count = axis_count(axis)
    return lax.ppermute(value, axis, [(i, i ^ mask) for i in range(count)])


def bit_masks(count):
    masks = []
    mask = 1
    while mask < count:
        masks.append(mask)
        mask *= 2
    return masks


def gather_dom(packed):
    count = lax.axis_size("dom")
    spread = jnp.broadcast_to(packed[None], (count,) + packed.shape)
    return lax.all_to_all(spread, "dom", 0, 0, tiled=True)


def reduce_scatter_dom(packed):
    return jnp.sum(lax.all_to_all(packed, "dom", 0, 0, tiled=True), axis=0)


def sum_sub(value):
    total = value
    for axis in reversed(SUB):
        count = lax.axis_size(axis)
        spread = jnp.broadcast_to(total[None], (count,) + total.shape)
        total = jnp.sum(lax.all_to_all(spread, axis, 0, 0, tiled=True), axis=0)
    return total


def gather_params(weights, gains):
    latent = weights[0].shape[1]
    gain_row = gains.reshape(1, -1)
    gain_row = jnp.pad(gain_row, ((0, 0), (0, latent - gain_row.shape[1])))
    packed = jnp.concatenate(list(weights) + [gain_row], axis=0)
    full = gather_dom(packed)
    count = full.shape[0]
    outs = []
    start = 0
    for w in weights:
        rows = w.shape[0]
        outs.append(full[:, start : start + rows].reshape(count * rows, latent))
        start += rows
    width = gains.shape[1]
    gain_full = full[:, start, : 2 * width].reshape(count, 2, width)
    gain_full = jnp.transpose(gain_full, (1, 0, 2)).reshape(2, count * width)
    outs.append(gain_full)
    return tuple(outs)


def reduce_params(parts, gain_terms, scale):
    count = lax.axis_size("dom")
    latent = parts[0].shape[1]
    blocks = [p.reshape(count, p.shape[0] // count, latent) for p in parts]
    width = gain_terms.shape[1] // count
    gain_block = jnp.transpose(gain_terms.reshape(2, count, width), (1, 0, 2)).reshape(count, 1, 2 * width)
    gain_block = jnp.pad(gain_block, ((0, 0), (0, 0), (0, latent - 2 * width)))
    packed = jnp.concatenate(blocks + [gain_block], axis=1)
    shard = reduce_scatter_dom(packed)
    shard = sum_sub(shard) * scale
    outs = []
    start = 0
    for b in blocks:
        rows = b.shape[1]
        outs.append(shard[start : start + rows])
        start += rows
    outs.append(shard[start, : 2 * width].reshape(2, width))
    return tuple(outs)


def one_hot(index, count):
    return (index[:, None] == jnp.arange(count, dtype=index.dtype)[None, :]).astype(jnp.bfloat16)


def select_rows(pick, table):
    if table.dtype == jnp.bfloat16:
        return jnp.dot(pick, table, preferred_element_type=jnp.float32).astype(jnp.bfloat16)
    return jnp.dot(
        pick.astype(jnp.float32), table, precision=lax.Precision.HIGHEST, preferred_element_type=jnp.float32
    )


def sum_rows(pick, values):
    return lax.dot_general(
        pick.astype(jnp.float32),
        values,
        (((0,), (0,)), ((), ())),
        precision=lax.Precision.HIGHEST,
        preferred_element_type=jnp.float32,
    )


def shards(
    node_feat,
    edge_feat,
    edge_dst,
    edge_dir,
    edge_count,
    w_edge_in,
    w_edge_out,
    w_node_in,
    w_node_out,
    gains,
    node_cot,
    edge_cot,
):
    full_edge_in, full_edge_out, full_node_in, full_node_out, full_gains = gather_params(
        (w_edge_in, w_edge_out, w_node_in, w_node_out), gains
    )
    gain_edge = full_gains[0].astype(jnp.float32)
    gain_node = full_gains[1].astype(jnp.float32)
    block_side = node_feat.shape[0]
    latent = node_feat.shape[2]
    padded_side = block_side + 2
    padded = with_halo(node_feat, (("dom", 0), (SUB, 1)), 1).reshape(
        padded_side * padded_side, latent
    )
    node_row = edge_dst // block_side
    node_col = edge_dst % block_side
    step_row = jnp.where(edge_dir == 0, 1, jnp.where(edge_dir == 1, -1, 0)).astype(jnp.int32)
    step_col = jnp.where(edge_dir == 2, 1, jnp.where(edge_dir == 3, -1, 0)).astype(jnp.int32)
    target_pad = (node_row + 1) * padded_side + node_col + 1
    source_pad = (node_row + 1 + step_row) * padded_side + node_col + 1 + step_col
    active = (jnp.arange(edge_dst.shape[0], dtype=jnp.int32) < edge_count[0]).astype(jnp.float32)[
        :, None
    ]
    padded_count = padded_side * padded_side
    pick_source = one_hot(source_pad, padded_count)
    pick_target = one_hot(target_pad, padded_count)
    pick_local = one_hot(edge_dst, block_side * block_side)
    inputs = jnp.concatenate(
        [edge_feat, select_rows(pick_source, padded), select_rows(pick_target, padded)], axis=1
    )
    pre_e, hidden_e, normed_e, inv_e, message = mlp_forward(
        inputs, full_edge_in, full_edge_out, gain_edge
    )
    aggregate = sum_rows(pick_local, message * active)
    node_rows = node_feat.reshape(block_side * block_side, latent)
    node_input = jnp.concatenate([node_rows, aggregate.astype(jnp.bfloat16)], axis=1)
    pre_n, hidden_n, normed_n, inv_n, _ = mlp_forward(
        node_input, full_node_in, full_node_out, gain_node
    )
    node_upstream = node_cot.reshape(block_side * block_side, latent).astype(jnp.float32)
    node_in_grad, node_first, node_second, node_gain = mlp_backward(
        node_upstream,
        node_input,
        pre_n,
        hidden_n,
        normed_n,
        inv_n,
        gain_node,
        full_node_in,
        full_node_out,
    )
    cot_float = edge_cot.astype(jnp.float32)
    upstream = active * (cot_float + select_rows(pick_local, node_in_grad[:, latent:]))
    edge_in_grad, edge_first, edge_second, edge_gain = mlp_backward(
        upstream, inputs, pre_e, hidden_e, normed_e, inv_e, gain_edge, full_edge_in, full_edge_out
    )
    edge_grad = (cot_float + edge_in_grad[:, :latent]).astype(jnp.bfloat16)
    spread = sum_rows(
        jnp.concatenate([pick_source, pick_target], axis=0),
        jnp.concatenate([edge_in_grad[:, latent : 2 * latent], edge_in_grad[:, 2 * latent :]], axis=0),
    )
    spread = spread.reshape(padded_side, padded_side, latent)
    outgoing = jnp.stack(
        [
            jnp.stack([spread[1:-1, 0], spread[0, 1:-1]]),
            jnp.stack([spread[-1, 1:-1], spread[1:-1, -1]]),
        ]
    )
    incoming = with_halo(outgoing.astype(jnp.bfloat16), (("dom", 0), (SUB, 1)), 1).astype(
        outgoing.dtype
    )
    inner = spread[1:-1, 1:-1]
    inner = inner.at[0].add(incoming[0, 1]).at[-1].add(incoming[3, 2])
    inner = inner.at[:, 0].add(incoming[2, 0]).at[:, -1].add(incoming[1, 3])
    node_total = node_upstream + node_in_grad[:, :latent]
    node_grad = (node_total.reshape(block_side, block_side, latent) + inner).astype(jnp.bfloat16)
    nodes_all = block_side * block_side * lax.axis_size("dom") * axis_count(SUB)
    grad_scale = lax.rsqrt(jnp.float32(nodes_all))
    results = reduce_params(
        (edge_first, edge_second, node_first, node_second), jnp.stack([edge_gain, node_gain]), grad_scale
    )
    return (node_grad, edge_grad) + results


def solution(mesh):
    in_specs = (
        P("dom", SUB, None),
        P(("dom",) + SUB, None),
        P(("dom",) + SUB),
        P(("dom",) + SUB),
        P(("dom",) + SUB),
        P("dom", None),
        P("dom", None),
        P("dom", None),
        P("dom", None),
        P(None, "dom"),
        P("dom", SUB, None),
        P(("dom",) + SUB, None),
    )
    out_specs = (
        P("dom", SUB, None),
        P(("dom",) + SUB, None),
        P("dom", None),
        P("dom", None),
        P("dom", None),
        P("dom", None),
        P(None, "dom"),
    )
    devices = mesh.devices
    low = 8 if devices.shape[1] % 8 == 0 else 1
    split = jax.sharding.Mesh(
        devices.reshape(devices.shape[0], devices.shape[1] // low, low), ("dom",) + SUB
    )
    return jax.shard_map(shards, mesh=split, in_specs=in_specs, out_specs=out_specs, check_vma=False)
```

```python
import jax
import jax.numpy as jnp
from jax import lax
from jax.sharding import PartitionSpec as P


def with_halo(block, sides, width):
    for axis, dim in sides:
        count = axis_count(axis)
        forward = [(i, i + 1) for i in range(count - 1)]
        backward = [(target, source) for source, target in forward]
        low = lax.ppermute(
            lax.slice_in_dim(block, block.shape[dim] - width, None, axis=dim), axis, forward
        )
        high = lax.ppermute(lax.slice_in_dim(block, 0, width, axis=dim), axis, backward)
        block = jnp.concatenate([low, block, high], axis=dim)
    return block


def layer_norm(raw_out):
    average = jnp.mean(raw_out, axis=-1, keepdims=True)
    centered = raw_out - average
    inv_std = lax.rsqrt(jnp.mean(centered * centered, axis=-1, keepdims=True) + 1e-05)
    return (centered * inv_std, inv_std)


def norm_back(upstream, normed, inv_std):
    return (
        upstream
        - jnp.mean(upstream, axis=-1, keepdims=True)
        - normed * jnp.mean(upstream * normed, axis=-1, keepdims=True)
    ) * inv_std


def mlp_forward(inputs, w_first, w_second, gain_vec):
    pre_act = jnp.dot(inputs, w_first, preferred_element_type=jnp.float32)
    hidden = jnp.maximum(pre_act, 0.0).astype(jnp.bfloat16)
    raw_out = jnp.dot(hidden, w_second, preferred_element_type=jnp.float32)
    normed, inv_std = layer_norm(raw_out)
    return (pre_act, hidden, normed, inv_std, normed * gain_vec)


def mlp_backward(upstream, inputs, pre_act, hidden, normed, inv_std, gain_vec, w_first, w_second):
    gain_part = jnp.sum(upstream * normed, axis=0)
    grad_raw = norm_back(upstream * gain_vec, normed, inv_std).astype(jnp.bfloat16)
    second_part = jnp.dot(hidden.T, grad_raw, preferred_element_type=jnp.float32)
    grad_hidden = jnp.dot(grad_raw, w_second.T, preferred_element_type=jnp.float32)
    grad_pre = jnp.where(pre_act > 0, grad_hidden, 0.0).astype(jnp.bfloat16)
    first_part = jnp.dot(inputs.T, grad_pre, preferred_element_type=jnp.float32)
    grad_inputs = jnp.dot(grad_pre, w_first.T, preferred_element_type=jnp.float32)
    return (grad_inputs, first_part, second_part, gain_part)


SUB = ("sub_hi", "sub_lo")


def axis_count(axis):
    if isinstance(axis, tuple):
        total = 1
        for name in axis:
            total *= lax.axis_size(name)
        return total
    return lax.axis_size(axis)


def exchange(value, axis, mask):
    count = axis_count(axis)
    return lax.ppermute(value, axis, [(i, i ^ mask) for i in range(count)])


def bit_masks(count):
    masks = []
    mask = 1
    while mask < count:
        masks.append(mask)
        mask *= 2
    return masks


def gather_dom(packed):
    count = lax.axis_size("dom")
    spread = jnp.broadcast_to(packed[None], (count,) + packed.shape)
    return lax.all_to_all(spread, "dom", 0, 0, tiled=True)


def reduce_scatter_dom(packed):
    return jnp.sum(lax.all_to_all(packed, "dom", 0, 0, tiled=True), axis=0)


def sum_sub(value):
    total = value
    for axis in reversed(SUB):
        count = lax.axis_size(axis)
        spread = jnp.broadcast_to(total[None], (count,) + total.shape)
        total = jnp.sum(lax.all_to_all(spread, axis, 0, 0, tiled=True), axis=0)
    return total


def gather_params(weights, gains):
    latent = weights[0].shape[1]
    gain_row = gains.reshape(1, -1)
    gain_row = jnp.pad(gain_row, ((0, 0), (0, latent - gain_row.shape[1])))
    packed = jnp.concatenate(list(weights) + [gain_row], axis=0)
    full = gather_dom(packed)
    count = full.shape[0]
    outs = []
    start = 0
    for w in weights:
        rows = w.shape[0]
        outs.append(full[:, start : start + rows].reshape(count * rows, latent))
        start += rows
    width = gains.shape[1]
    gain_full = full[:, start, : 2 * width].reshape(count, 2, width)
    gain_full = jnp.transpose(gain_full, (1, 0, 2)).reshape(2, count * width)
    outs.append(gain_full)
    return tuple(outs)


def reduce_params(parts, gain_terms, scale):
    count = lax.axis_size("dom")
    latent = parts[0].shape[1]
    blocks = [p.reshape(count, p.shape[0] // count, latent) for p in parts]
    width = gain_terms.shape[1] // count
    gain_block = jnp.transpose(gain_terms.reshape(2, count, width), (1, 0, 2)).reshape(count, 1, 2 * width)
    gain_block = jnp.pad(gain_block, ((0, 0), (0, 0), (0, latent - 2 * width)))
    packed = jnp.concatenate(blocks + [gain_block], axis=1)
    shard = reduce_scatter_dom(packed)
    shard = sum_sub(shard) * scale
    outs = []
    start = 0
    for b in blocks:
        rows = b.shape[1]
        outs.append(shard[start : start + rows])
        start += rows
    outs.append(shard[start, : 2 * width].reshape(2, width))
    return tuple(outs)


def shift_in(value, axis, step):
    count = axis_count(axis)
    if step > 0:
        pairs = [(i, i + 1) for i in range(count - 1)]
    else:
        pairs = [(i + 1, i) for i in range(count - 1)]
    return lax.ppermute(value.astype(jnp.bfloat16), axis, pairs).astype(value.dtype)


def one_hot(index, count):
    return (index[:, None] == jnp.arange(count, dtype=index.dtype)[None, :]).astype(jnp.bfloat16)


def select_rows(pick, table):
    if table.dtype == jnp.bfloat16:
        return jnp.dot(pick, table, preferred_element_type=jnp.float32).astype(jnp.bfloat16)
    return jnp.dot(
        pick.astype(jnp.float32), table, precision=lax.Precision.HIGHEST, preferred_element_type=jnp.float32
    )


def sum_rows(pick, values):
    return lax.dot_general(
        pick.astype(jnp.float32),
        values,
        (((0,), (0,)), ((), ())),
        precision=lax.Precision.HIGHEST,
        preferred_element_type=jnp.float32,
    )


def shards(
    node_feat,
    edge_feat,
    edge_dst,
    edge_dir,
    edge_count,
    w_edge_in,
    w_edge_out,
    w_node_in,
    w_node_out,
    gains,
    node_cot,
    edge_cot,
):
    full_edge_in, full_edge_out, full_node_in, full_node_out, full_gains = gather_params(
        (w_edge_in, w_edge_out, w_node_in, w_node_out), gains
    )
    gain_edge = full_gains[0].astype(jnp.float32)
    gain_node = full_gains[1].astype(jnp.float32)
    block_side = node_feat.shape[0]
    latent = node_feat.shape[2]
    padded_side = block_side + 2
    top = shift_in(node_feat[-1], "dom", 1)
    bottom = shift_in(node_feat[0], "dom", -1)
    left = shift_in(node_feat[:, -1], SUB, 1)
    right = shift_in(node_feat[:, 0], SUB, -1)
    middle = jnp.concatenate([left[:, None], node_feat, right[:, None]], axis=1)
    edge_rows = jnp.pad(jnp.stack([top, bottom]), ((0, 0), (1, 1), (0, 0)))
    padded = jnp.concatenate([edge_rows[:1], middle, edge_rows[1:]], axis=0).reshape(
        padded_side * padded_side, latent
    )
    node_row = edge_dst // block_side
    node_col = edge_dst % block_side
    step_row = jnp.where(edge_dir == 0, 1, jnp.where(edge_dir == 1, -1, 0)).astype(jnp.int32)
    step_col = jnp.where(edge_dir == 2, 1, jnp.where(edge_dir == 3, -1, 0)).astype(jnp.int32)
    target_pad = (node_row + 1) * padded_side + node_col + 1
    source_pad = (node_row + 1 + step_row) * padded_side + node_col + 1 + step_col
    active = (jnp.arange(edge_dst.shape[0], dtype=jnp.int32) < edge_count[0]).astype(jnp.float32)[
        :, None
    ]
    padded_count = padded_side * padded_side
    pick_source = one_hot(source_pad, padded_count)
    pick_target = one_hot(target_pad, padded_count)
    pick_local = one_hot(edge_dst, block_side * block_side)
    inputs = jnp.concatenate(
        [edge_feat, select_rows(pick_source, padded), select_rows(pick_target, padded)], axis=1
    )
    pre_e, hidden_e, normed_e, inv_e, message = mlp_forward(
        inputs, full_edge_in, full_edge_out, gain_edge
    )
    aggregate = sum_rows(pick_local, message * active)
    node_rows = node_feat.reshape(block_side * block_side, latent)
    node_input = jnp.concatenate([node_rows, aggregate.astype(jnp.bfloat16)], axis=1)
    pre_n, hidden_n, normed_n, inv_n, _ = mlp_forward(
        node_input, full_node_in, full_node_out, gain_node
    )
    node_upstream = node_cot.reshape(block_side * block_side, latent).astype(jnp.float32)
    node_in_grad, node_first, node_second, node_gain = mlp_backward(
        node_upstream,
        node_input,
        pre_n,
        hidden_n,
        normed_n,
        inv_n,
        gain_node,
        full_node_in,
        full_node_out,
    )
    cot_float = edge_cot.astype(jnp.float32)
    upstream = active * (cot_float + select_rows(pick_local, node_in_grad[:, latent:]))
    edge_in_grad, edge_first, edge_second, edge_gain = mlp_backward(
        upstream, inputs, pre_e, hidden_e, normed_e, inv_e, gain_edge, full_edge_in, full_edge_out
    )
    edge_grad = (cot_float + edge_in_grad[:, :latent]).astype(jnp.bfloat16)
    spread = sum_rows(
        jnp.concatenate([pick_source, pick_target], axis=0),
        jnp.concatenate([edge_in_grad[:, latent : 2 * latent], edge_in_grad[:, 2 * latent :]], axis=0),
    )
    spread = spread.reshape(padded_side, padded_side, latent)
    inner = spread[1:-1, 1:-1]
    from_prev_dom = shift_in(spread[-1, 1:-1], "dom", 1)
    from_next_dom = shift_in(spread[0, 1:-1], "dom", -1)
    from_prev_sub = shift_in(spread[1:-1, -1], SUB, 1)
    from_next_sub = shift_in(spread[1:-1, 0], SUB, -1)
    inner = inner.at[0].add(from_prev_dom).at[-1].add(from_next_dom)
    inner = inner.at[:, 0].add(from_prev_sub).at[:, -1].add(from_next_sub)
    node_total = node_upstream + node_in_grad[:, :latent]
    node_grad = (node_total.reshape(block_side, block_side, latent) + inner).astype(jnp.bfloat16)
    nodes_all = block_side * block_side * lax.axis_size("dom") * axis_count(SUB)
    grad_scale = lax.rsqrt(jnp.float32(nodes_all))
    results = reduce_params(
        (edge_first, edge_second, node_first, node_second), jnp.stack([edge_gain, node_gain]), grad_scale
    )
    return (node_grad, edge_grad) + results


def solution(mesh):
    in_specs = (
        P("dom", SUB, None),
        P(("dom",) + SUB, None),
        P(("dom",) + SUB),
        P(("dom",) + SUB),
        P(("dom",) + SUB),
        P("dom", None),
        P("dom", None),
        P("dom", None),
        P("dom", None),
        P(None, "dom"),
        P("dom", SUB, None),
        P(("dom",) + SUB, None),
    )
    out_specs = (
        P("dom", SUB, None),
        P(("dom",) + SUB, None),
        P("dom", None),
        P("dom", None),
        P("dom", None),
        P("dom", None),
        P(None, "dom"),
    )
    devices = mesh.devices
    low = 8 if devices.shape[1] % 8 == 0 else 1
    split = jax.sharding.Mesh(
        devices.reshape(devices.shape[0], devices.shape[1] // low, low), ("dom",) + SUB
    )
    return jax.shard_map(shards, mesh=split, in_specs=in_specs, out_specs=out_specs, check_vma=False)
```

```python
import jax
import jax.numpy as jnp
from jax import lax
from jax.sharding import PartitionSpec as P


def with_halo(block, sides, width):
    for axis, dim in sides:
        count = axis_count(axis)
        forward = [(i, i + 1) for i in range(count - 1)]
        backward = [(target, source) for source, target in forward]
        low = lax.ppermute(
            lax.slice_in_dim(block, block.shape[dim] - width, None, axis=dim), axis, forward
        )
        high = lax.ppermute(lax.slice_in_dim(block, 0, width, axis=dim), axis, backward)
        block = jnp.concatenate([low, block, high], axis=dim)
    return block


def layer_norm(raw_out):
    average = jnp.mean(raw_out, axis=-1, keepdims=True)
    centered = raw_out - average
    inv_std = lax.rsqrt(jnp.mean(centered * centered, axis=-1, keepdims=True) + 1e-05)
    return (centered * inv_std, inv_std)


def norm_back(upstream, normed, inv_std):
    return (
        upstream
        - jnp.mean(upstream, axis=-1, keepdims=True)
        - normed * jnp.mean(upstream * normed, axis=-1, keepdims=True)
    ) * inv_std


def mlp_forward(inputs, w_first, w_second, gain_vec):
    pre_act = jnp.dot(inputs, w_first, preferred_element_type=jnp.float32)
    hidden = jnp.maximum(pre_act, 0.0).astype(jnp.bfloat16)
    raw_out = jnp.dot(hidden, w_second, preferred_element_type=jnp.float32)
    normed, inv_std = layer_norm(raw_out)
    return (pre_act, hidden, normed, inv_std, normed * gain_vec)


def mlp_backward(upstream, inputs, pre_act, hidden, normed, inv_std, gain_vec, w_first, w_second):
    gain_part = jnp.sum(upstream * normed, axis=0)
    grad_raw = norm_back(upstream * gain_vec, normed, inv_std).astype(jnp.bfloat16)
    second_part = jnp.dot(hidden.T, grad_raw, preferred_element_type=jnp.float32)
    grad_hidden = jnp.dot(grad_raw, w_second.T, preferred_element_type=jnp.float32)
    grad_pre = jnp.where(pre_act > 0, grad_hidden, 0.0).astype(jnp.bfloat16)
    first_part = jnp.dot(inputs.T, grad_pre, preferred_element_type=jnp.float32)
    grad_inputs = jnp.dot(grad_pre, w_first.T, preferred_element_type=jnp.float32)
    return (grad_inputs, first_part, second_part, gain_part)


SUB = ("sub_hi", "sub_lo")


def axis_count(axis):
    if isinstance(axis, tuple):
        total = 1
        for name in axis:
            total *= lax.axis_size(name)
        return total
    return lax.axis_size(axis)


def exchange(value, axis, mask):
    count = axis_count(axis)
    return lax.ppermute(value, axis, [(i, i ^ mask) for i in range(count)])


def bit_masks(count):
    masks = []
    mask = 1
    while mask < count:
        masks.append(mask)
        mask *= 2
    return masks


def gather_dom(packed):
    count = lax.axis_size("dom")
    spread = jnp.broadcast_to(packed[None], (count,) + packed.shape)
    return lax.all_to_all(spread, "dom", 0, 0, tiled=True)


def reduce_scatter_dom(packed):
    pieces = lax.all_to_all(packed.astype(jnp.bfloat16), "dom", 0, 0, tiled=True)
    return jnp.sum(pieces.astype(jnp.float32), axis=0)


def sum_sub(value):
    total = value
    for axis in reversed(SUB):
        count = lax.axis_size(axis)
        spread = jnp.broadcast_to(total.astype(jnp.bfloat16)[None], (count,) + total.shape)
        gathered = lax.all_to_all(spread, axis, 0, 0, tiled=True)
        total = jnp.sum(gathered.astype(jnp.float32), axis=0)
    return total


def gather_params(weights, gains):
    latent = weights[0].shape[1]
    gain_row = gains.reshape(1, -1)
    gain_row = jnp.pad(gain_row, ((0, 0), (0, latent - gain_row.shape[1])))
    packed = jnp.concatenate(list(weights) + [gain_row], axis=0)
    full = gather_dom(packed)
    count = full.shape[0]
    outs = []
    start = 0
    for w in weights:
        rows = w.shape[0]
        outs.append(full[:, start : start + rows].reshape(count * rows, latent))
        start += rows
    width = gains.shape[1]
    gain_full = full[:, start, : 2 * width].reshape(count, 2, width)
    gain_full = jnp.transpose(gain_full, (1, 0, 2)).reshape(2, count * width)
    outs.append(gain_full)
    return tuple(outs)


def reduce_params(parts, gain_terms, scale):
    count = lax.axis_size("dom")
    latent = parts[0].shape[1]
    blocks = [p.reshape(count, p.shape[0] // count, latent) for p in parts]
    width = gain_terms.shape[1] // count
    gain_block = jnp.transpose(gain_terms.reshape(2, count, width), (1, 0, 2)).reshape(count, 1, 2 * width)
    gain_block = jnp.pad(gain_block, ((0, 0), (0, 0), (0, latent - 2 * width)))
    packed = jnp.concatenate(blocks + [gain_block], axis=1)
    shard = reduce_scatter_dom(packed)
    shard = sum_sub(shard) * scale
    outs = []
    start = 0
    for b in blocks:
        rows = b.shape[1]
        outs.append(shard[start : start + rows])
        start += rows
    outs.append(shard[start, : 2 * width].reshape(2, width))
    return tuple(outs)


def shift_in(value, axis, step):
    count = axis_count(axis)
    if step > 0:
        pairs = [(i, i + 1) for i in range(count - 1)]
    else:
        pairs = [(i + 1, i) for i in range(count - 1)]
    return lax.ppermute(value.astype(jnp.bfloat16), axis, pairs).astype(value.dtype)


def one_hot(index, count):
    return (index[:, None] == jnp.arange(count, dtype=index.dtype)[None, :]).astype(jnp.bfloat16)


def select_rows(pick, table):
    if table.dtype == jnp.bfloat16:
        return jnp.dot(pick, table, preferred_element_type=jnp.float32).astype(jnp.bfloat16)
    return jnp.dot(
        pick.astype(jnp.float32), table, precision=lax.Precision.HIGHEST, preferred_element_type=jnp.float32
    )


def sum_rows(pick, values):
    return lax.dot_general(
        pick.astype(jnp.float32),
        values,
        (((0,), (0,)), ((), ())),
        precision=lax.Precision.HIGHEST,
        preferred_element_type=jnp.float32,
    )


def shards(
    node_feat,
    edge_feat,
    edge_dst,
    edge_dir,
    edge_count,
    w_edge_in,
    w_edge_out,
    w_node_in,
    w_node_out,
    gains,
    node_cot,
    edge_cot,
):
    full_edge_in, full_edge_out, full_node_in, full_node_out, full_gains = gather_params(
        (w_edge_in, w_edge_out, w_node_in, w_node_out), gains
    )
    gain_edge = full_gains[0].astype(jnp.float32)
    gain_node = full_gains[1].astype(jnp.float32)
    block_side = node_feat.shape[0]
    latent = node_feat.shape[2]
    padded_side = block_side + 2
    top = shift_in(node_feat[-1], "dom", 1)
    bottom = shift_in(node_feat[0], "dom", -1)
    left = shift_in(node_feat[:, -1], SUB, 1)
    right = shift_in(node_feat[:, 0], SUB, -1)
    middle = jnp.concatenate([left[:, None], node_feat, right[:, None]], axis=1)
    edge_rows = jnp.pad(jnp.stack([top, bottom]), ((0, 0), (1, 1), (0, 0)))
    padded = jnp.concatenate([edge_rows[:1], middle, edge_rows[1:]], axis=0).reshape(
        padded_side * padded_side, latent
    )
    node_row = edge_dst // block_side
    node_col = edge_dst % block_side
    step_row = jnp.where(edge_dir == 0, 1, jnp.where(edge_dir == 1, -1, 0)).astype(jnp.int32)
    step_col = jnp.where(edge_dir == 2, 1, jnp.where(edge_dir == 3, -1, 0)).astype(jnp.int32)
    target_pad = (node_row + 1) * padded_side + node_col + 1
    source_pad = (node_row + 1 + step_row) * padded_side + node_col + 1 + step_col
    active = (jnp.arange(edge_dst.shape[0], dtype=jnp.int32) < edge_count[0]).astype(jnp.float32)[
        :, None
    ]
    padded_count = padded_side * padded_side
    pick_source = one_hot(source_pad, padded_count)
    pick_target = one_hot(target_pad, padded_count)
    pick_local = one_hot(edge_dst, block_side * block_side)
    inputs = jnp.concatenate(
        [edge_feat, select_rows(pick_source, padded), select_rows(pick_target, padded)], axis=1
    )
    pre_e, hidden_e, normed_e, inv_e, message = mlp_forward(
        inputs, full_edge_in, full_edge_out, gain_edge
    )
    aggregate = sum_rows(pick_local, message * active)
    node_rows = node_feat.reshape(block_side * block_side, latent)
    node_input = jnp.concatenate([node_rows, aggregate.astype(jnp.bfloat16)], axis=1)
    pre_n, hidden_n, normed_n, inv_n, _ = mlp_forward(
        node_input, full_node_in, full_node_out, gain_node
    )
    node_upstream = node_cot.reshape(block_side * block_side, latent).astype(jnp.float32)
    node_in_grad, node_first, node_second, node_gain = mlp_backward(
        node_upstream,
        node_input,
        pre_n,
        hidden_n,
        normed_n,
        inv_n,
        gain_node,
        full_node_in,
        full_node_out,
    )
    cot_float = edge_cot.astype(jnp.float32)
    upstream = active * (cot_float + select_rows(pick_local, node_in_grad[:, latent:]))
    edge_in_grad, edge_first, edge_second, edge_gain = mlp_backward(
        upstream, inputs, pre_e, hidden_e, normed_e, inv_e, gain_edge, full_edge_in, full_edge_out
    )
    edge_grad = (cot_float + edge_in_grad[:, :latent]).astype(jnp.bfloat16)
    spread = sum_rows(
        jnp.concatenate([pick_source, pick_target], axis=0),
        jnp.concatenate([edge_in_grad[:, latent : 2 * latent], edge_in_grad[:, 2 * latent :]], axis=0),
    )
    spread = spread.reshape(padded_side, padded_side, latent)
    inner = spread[1:-1, 1:-1]
    from_prev_dom = shift_in(spread[-1, 1:-1], "dom", 1)
    from_next_dom = shift_in(spread[0, 1:-1], "dom", -1)
    from_prev_sub = shift_in(spread[1:-1, -1], SUB, 1)
    from_next_sub = shift_in(spread[1:-1, 0], SUB, -1)
    inner = inner.at[0].add(from_prev_dom).at[-1].add(from_next_dom)
    inner = inner.at[:, 0].add(from_prev_sub).at[:, -1].add(from_next_sub)
    node_total = node_upstream + node_in_grad[:, :latent]
    node_grad = (node_total.reshape(block_side, block_side, latent) + inner).astype(jnp.bfloat16)
    nodes_all = block_side * block_side * lax.axis_size("dom") * axis_count(SUB)
    grad_scale = lax.rsqrt(jnp.float32(nodes_all))
    results = reduce_params(
        (edge_first, edge_second, node_first, node_second), jnp.stack([edge_gain, node_gain]), grad_scale
    )
    return (node_grad, edge_grad) + results


def solution(mesh):
    in_specs = (
        P("dom", SUB, None),
        P(("dom",) + SUB, None),
        P(("dom",) + SUB),
        P(("dom",) + SUB),
        P(("dom",) + SUB),
        P("dom", None),
        P("dom", None),
        P("dom", None),
        P("dom", None),
        P(None, "dom"),
        P("dom", SUB, None),
        P(("dom",) + SUB, None),
    )
    out_specs = (
        P("dom", SUB, None),
        P(("dom",) + SUB, None),
        P("dom", None),
        P("dom", None),
        P("dom", None),
        P("dom", None),
        P(None, "dom"),
    )
    devices = mesh.devices
    low = 8 if devices.shape[1] % 8 == 0 else 1
    split = jax.sharding.Mesh(
        devices.reshape(devices.shape[0], devices.shape[1] // low, low), ("dom",) + SUB
    )
    return jax.shard_map(shards, mesh=split, in_specs=in_specs, out_specs=out_specs, check_vma=False)
```

```python
import jax
import jax.numpy as jnp
from jax import lax
from jax.sharding import PartitionSpec as P


def with_halo(block, sides, width):
    for axis, dim in sides:
        count = axis_count(axis)
        forward = [(i, i + 1) for i in range(count - 1)]
        backward = [(target, source) for source, target in forward]
        low = lax.ppermute(
            lax.slice_in_dim(block, block.shape[dim] - width, None, axis=dim), axis, forward
        )
        high = lax.ppermute(lax.slice_in_dim(block, 0, width, axis=dim), axis, backward)
        block = jnp.concatenate([low, block, high], axis=dim)
    return block


def layer_norm(raw_out):
    average = jnp.mean(raw_out, axis=-1, keepdims=True)
    centered = raw_out - average
    inv_std = lax.rsqrt(jnp.mean(centered * centered, axis=-1, keepdims=True) + 1e-05)
    return (centered * inv_std, inv_std)


def norm_back(upstream, normed, inv_std):
    return (
        upstream
        - jnp.mean(upstream, axis=-1, keepdims=True)
        - normed * jnp.mean(upstream * normed, axis=-1, keepdims=True)
    ) * inv_std


def mlp_forward(inputs, w_first, w_second, gain_vec):
    pre_act = jnp.dot(inputs, w_first, preferred_element_type=jnp.float32)
    hidden = jnp.maximum(pre_act, 0.0).astype(jnp.bfloat16)
    raw_out = jnp.dot(hidden, w_second, preferred_element_type=jnp.float32)
    normed, inv_std = layer_norm(raw_out)
    return (pre_act, hidden, normed, inv_std, normed * gain_vec)


def mlp_backward(upstream, inputs, pre_act, hidden, normed, inv_std, gain_vec, w_first, w_second):
    gain_part = jnp.sum(upstream * normed, axis=0)
    grad_raw = norm_back(upstream * gain_vec, normed, inv_std).astype(jnp.bfloat16)
    second_part = jnp.dot(hidden.T, grad_raw, preferred_element_type=jnp.float32)
    grad_hidden = jnp.dot(grad_raw, w_second.T, preferred_element_type=jnp.float32)
    grad_pre = jnp.where(pre_act > 0, grad_hidden, 0.0).astype(jnp.bfloat16)
    first_part = jnp.dot(inputs.T, grad_pre, preferred_element_type=jnp.float32)
    grad_inputs = jnp.dot(grad_pre, w_first.T, preferred_element_type=jnp.float32)
    return (grad_inputs, first_part, second_part, gain_part)


SUB = ("sub_hi", "sub_lo")


def axis_count(axis):
    if isinstance(axis, tuple):
        total = 1
        for name in axis:
            total *= lax.axis_size(name)
        return total
    return lax.axis_size(axis)


def exchange(value, axis, mask):
    count = axis_count(axis)
    return lax.ppermute(value, axis, [(i, i ^ mask) for i in range(count)])


def bit_masks(count):
    masks = []
    mask = 1
    while mask < count:
        masks.append(mask)
        mask *= 2
    return masks


def gather_dom(packed):
    count = lax.axis_size("dom")
    spread = jnp.broadcast_to(packed[None], (count,) + packed.shape)
    return lax.all_to_all(spread, "dom", 0, 0, tiled=True)


def reduce_scatter_dom(packed):
    return jnp.sum(lax.all_to_all(packed, "dom", 0, 0, tiled=True), axis=0)


def sum_sub(value):
    total = value
    for axis in reversed(SUB):
        count = lax.axis_size(axis)
        spread = jnp.broadcast_to(total[None], (count,) + total.shape)
        total = jnp.sum(lax.all_to_all(spread, axis, 0, 0, tiled=True), axis=0)
    return total


def gather_params(weights, gains, first_row, last_row):
    latent = weights[0].shape[1]
    count = lax.axis_size("dom")
    index = lax.axis_index("dom")
    gain_row = gains.reshape(1, -1)
    gain_row = jnp.pad(gain_row, ((0, 0), (0, latent - gain_row.shape[1])))
    packed = jnp.concatenate(list(weights) + [gain_row], axis=0)
    target = jnp.arange(count)[:, None, None]
    edge_rows = jnp.where(target == index + 1, last_row[None], jnp.where(target == index - 1, first_row[None], 0))
    spread = jnp.concatenate(
        [jnp.broadcast_to(packed[None], (count,) + packed.shape), edge_rows.astype(packed.dtype)], axis=1
    )
    received = lax.all_to_all(spread, "dom", 0, 0, tiled=True)
    rows = packed.shape[0]
    top = lax.dynamic_index_in_dim(received, (index + count - 1) % count, keepdims=False)[rows:]
    bottom = lax.dynamic_index_in_dim(received, (index + 1) % count, keepdims=False)[rows:]
    full = received[:, :rows]
    outs = []
    start = 0
    for w in weights:
        part = w.shape[0]
        outs.append(full[:, start : start + part].reshape(count * part, latent))
        start += part
    width = gains.shape[1]
    gain_full = full[:, start, : 2 * width].reshape(count, 2, width)
    gain_full = jnp.transpose(gain_full, (1, 0, 2)).reshape(2, count * width)
    outs.append(gain_full)
    return tuple(outs), top, bottom


def reduce_params(parts, gain_terms, scale):
    count = lax.axis_size("dom")
    latent = parts[0].shape[1]
    blocks = [p.reshape(count, p.shape[0] // count, latent) for p in parts]
    width = gain_terms.shape[1] // count
    gain_block = jnp.transpose(gain_terms.reshape(2, count, width), (1, 0, 2)).reshape(count, 1, 2 * width)
    gain_block = jnp.pad(gain_block, ((0, 0), (0, 0), (0, latent - 2 * width)))
    packed = jnp.concatenate(blocks + [gain_block], axis=1)
    shard = reduce_scatter_dom(packed)
    shard = sum_sub(shard) * scale
    outs = []
    start = 0
    for b in blocks:
        rows = b.shape[1]
        outs.append(shard[start : start + rows])
        start += rows
    outs.append(shard[start, : 2 * width].reshape(2, width))
    return tuple(outs)


def shift_in(value, axis, step):
    count = axis_count(axis)
    if step > 0:
        pairs = [(i, i + 1) for i in range(count - 1)]
    else:
        pairs = [(i + 1, i) for i in range(count - 1)]
    return lax.ppermute(value.astype(jnp.bfloat16), axis, pairs).astype(value.dtype)


def one_hot(index, count):
    return (index[:, None] == jnp.arange(count, dtype=index.dtype)[None, :]).astype(jnp.bfloat16)


def select_rows(pick, table):
    if table.dtype == jnp.bfloat16:
        return jnp.dot(pick, table, preferred_element_type=jnp.float32).astype(jnp.bfloat16)
    return jnp.dot(
        pick.astype(jnp.float32), table, precision=lax.Precision.HIGHEST, preferred_element_type=jnp.float32
    )


def sum_rows(pick, values):
    return lax.dot_general(
        pick.astype(jnp.float32),
        values,
        (((0,), (0,)), ((), ())),
        precision=lax.Precision.HIGHEST,
        preferred_element_type=jnp.float32,
    )


def shards(
    node_feat,
    edge_feat,
    edge_dst,
    edge_dir,
    edge_count,
    w_edge_in,
    w_edge_out,
    w_node_in,
    w_node_out,
    gains,
    node_cot,
    edge_cot,
):
    (full_edge_in, full_edge_out, full_node_in, full_node_out, full_gains), top, bottom = gather_params(
        (w_edge_in, w_edge_out, w_node_in, w_node_out), gains, node_feat[0], node_feat[-1]
    )
    gain_edge = full_gains[0].astype(jnp.float32)
    gain_node = full_gains[1].astype(jnp.float32)
    block_side = node_feat.shape[0]
    latent = node_feat.shape[2]
    padded_side = block_side + 2
    left = shift_in(node_feat[:, -1], SUB, 1)
    right = shift_in(node_feat[:, 0], SUB, -1)
    middle = jnp.concatenate([left[:, None], node_feat, right[:, None]], axis=1)
    edge_rows = jnp.pad(jnp.stack([top, bottom]), ((0, 0), (1, 1), (0, 0)))
    padded = jnp.concatenate([edge_rows[:1], middle, edge_rows[1:]], axis=0).reshape(
        padded_side * padded_side, latent
    )
    node_row = edge_dst // block_side
    node_col = edge_dst % block_side
    step_row = jnp.where(edge_dir == 0, 1, jnp.where(edge_dir == 1, -1, 0)).astype(jnp.int32)
    step_col = jnp.where(edge_dir == 2, 1, jnp.where(edge_dir == 3, -1, 0)).astype(jnp.int32)
    target_pad = (node_row + 1) * padded_side + node_col + 1
    source_pad = (node_row + 1 + step_row) * padded_side + node_col + 1 + step_col
    active = (jnp.arange(edge_dst.shape[0], dtype=jnp.int32) < edge_count[0]).astype(jnp.float32)[
        :, None
    ]
    padded_count = padded_side * padded_side
    pick_source = one_hot(source_pad, padded_count)
    pick_target = one_hot(target_pad, padded_count)
    pick_local = one_hot(edge_dst, block_side * block_side)
    inputs = jnp.concatenate(
        [edge_feat, select_rows(pick_source, padded), select_rows(pick_target, padded)], axis=1
    )
    pre_e, hidden_e, normed_e, inv_e, message = mlp_forward(
        inputs, full_edge_in, full_edge_out, gain_edge
    )
    aggregate = sum_rows(pick_local, message * active)
    node_rows = node_feat.reshape(block_side * block_side, latent)
    node_input = jnp.concatenate([node_rows, aggregate.astype(jnp.bfloat16)], axis=1)
    pre_n, hidden_n, normed_n, inv_n, _ = mlp_forward(
        node_input, full_node_in, full_node_out, gain_node
    )
    node_upstream = node_cot.reshape(block_side * block_side, latent).astype(jnp.float32)
    node_in_grad, node_first, node_second, node_gain = mlp_backward(
        node_upstream,
        node_input,
        pre_n,
        hidden_n,
        normed_n,
        inv_n,
        gain_node,
        full_node_in,
        full_node_out,
    )
    cot_float = edge_cot.astype(jnp.float32)
    upstream = active * (cot_float + select_rows(pick_local, node_in_grad[:, latent:]))
    edge_in_grad, edge_first, edge_second, edge_gain = mlp_backward(
        upstream, inputs, pre_e, hidden_e, normed_e, inv_e, gain_edge, full_edge_in, full_edge_out
    )
    edge_grad = (cot_float + edge_in_grad[:, :latent]).astype(jnp.bfloat16)
    spread = sum_rows(
        jnp.concatenate([pick_source, pick_target], axis=0),
        jnp.concatenate([edge_in_grad[:, latent : 2 * latent], edge_in_grad[:, 2 * latent :]], axis=0),
    )
    spread = spread.reshape(padded_side, padded_side, latent)
    inner = spread[1:-1, 1:-1]
    from_prev_dom = shift_in(spread[-1, 1:-1], "dom", 1)
    from_next_dom = shift_in(spread[0, 1:-1], "dom", -1)
    from_prev_sub = shift_in(spread[1:-1, -1], SUB, 1)
    from_next_sub = shift_in(spread[1:-1, 0], SUB, -1)
    inner = inner.at[0].add(from_prev_dom).at[-1].add(from_next_dom)
    inner = inner.at[:, 0].add(from_prev_sub).at[:, -1].add(from_next_sub)
    node_total = node_upstream + node_in_grad[:, :latent]
    node_grad = (node_total.reshape(block_side, block_side, latent) + inner).astype(jnp.bfloat16)
    nodes_all = block_side * block_side * lax.axis_size("dom") * axis_count(SUB)
    grad_scale = lax.rsqrt(jnp.float32(nodes_all))
    results = reduce_params(
        (edge_first, edge_second, node_first, node_second), jnp.stack([edge_gain, node_gain]), grad_scale
    )
    return (node_grad, edge_grad) + results


def solution(mesh):
    in_specs = (
        P("dom", SUB, None),
        P(("dom",) + SUB, None),
        P(("dom",) + SUB),
        P(("dom",) + SUB),
        P(("dom",) + SUB),
        P("dom", None),
        P("dom", None),
        P("dom", None),
        P("dom", None),
        P(None, "dom"),
        P("dom", SUB, None),
        P(("dom",) + SUB, None),
    )
    out_specs = (
        P("dom", SUB, None),
        P(("dom",) + SUB, None),
        P("dom", None),
        P("dom", None),
        P("dom", None),
        P("dom", None),
        P(None, "dom"),
    )
    devices = mesh.devices
    low = 8 if devices.shape[1] % 8 == 0 else 1
    split = jax.sharding.Mesh(
        devices.reshape(devices.shape[0], devices.shape[1] // low, low), ("dom",) + SUB
    )
    return jax.shard_map(shards, mesh=split, in_specs=in_specs, out_specs=out_specs, check_vma=False)
```

```python
import jax
import jax.numpy as jnp
from jax import lax
from jax.sharding import PartitionSpec as P


def with_halo(block, sides, width):
    for axis, dim in sides:
        count = axis_count(axis)
        forward = [(i, i + 1) for i in range(count - 1)]
        backward = [(target, source) for source, target in forward]
        low = lax.ppermute(
            lax.slice_in_dim(block, block.shape[dim] - width, None, axis=dim), axis, forward
        )
        high = lax.ppermute(lax.slice_in_dim(block, 0, width, axis=dim), axis, backward)
        block = jnp.concatenate([low, block, high], axis=dim)
    return block


def layer_norm(raw_out):
    average = jnp.mean(raw_out, axis=-1, keepdims=True)
    centered = raw_out - average
    inv_std = lax.rsqrt(jnp.mean(centered * centered, axis=-1, keepdims=True) + 1e-05)
    return (centered * inv_std, inv_std)


def norm_back(upstream, normed, inv_std):
    return (
        upstream
        - jnp.mean(upstream, axis=-1, keepdims=True)
        - normed * jnp.mean(upstream * normed, axis=-1, keepdims=True)
    ) * inv_std


def mlp_forward(inputs, w_first, w_second, gain_vec):
    pre_act = jnp.dot(inputs, w_first, preferred_element_type=jnp.float32)
    hidden = jnp.maximum(pre_act, 0.0).astype(jnp.bfloat16)
    raw_out = jnp.dot(hidden, w_second, preferred_element_type=jnp.float32)
    normed, inv_std = layer_norm(raw_out)
    return (pre_act, hidden, normed, inv_std, normed * gain_vec)


def mlp_backward(upstream, inputs, pre_act, hidden, normed, inv_std, gain_vec, w_first, w_second):
    gain_part = jnp.sum(upstream * normed, axis=0)
    grad_raw = norm_back(upstream * gain_vec, normed, inv_std).astype(jnp.bfloat16)
    second_part = jnp.dot(hidden.T, grad_raw, preferred_element_type=jnp.float32)
    grad_hidden = jnp.dot(grad_raw, w_second.T, preferred_element_type=jnp.float32)
    grad_pre = jnp.where(pre_act > 0, grad_hidden, 0.0).astype(jnp.bfloat16)
    first_part = jnp.dot(inputs.T, grad_pre, preferred_element_type=jnp.float32)
    grad_inputs = jnp.dot(grad_pre, w_first.T, preferred_element_type=jnp.float32)
    return (grad_inputs, first_part, second_part, gain_part)


SUB = ("sub_hi", "sub_lo")


def axis_count(axis):
    if isinstance(axis, tuple):
        total = 1
        for name in axis:
            total *= lax.axis_size(name)
        return total
    return lax.axis_size(axis)


def exchange(value, axis, mask):
    count = axis_count(axis)
    return lax.ppermute(value, axis, [(i, i ^ mask) for i in range(count)])


def bit_masks(count):
    masks = []
    mask = 1
    while mask < count:
        masks.append(mask)
        mask *= 2
    return masks


def gather_dom(packed):
    count = lax.axis_size("dom")
    spread = jnp.broadcast_to(packed[None], (count,) + packed.shape)
    return lax.all_to_all(spread, "dom", 0, 0, tiled=True)


def reduce_scatter_dom(packed):
    return jnp.sum(lax.all_to_all(packed, "dom", 0, 0, tiled=True), axis=0)


def sum_sub(value):
    total = value
    for axis in SUB:
        count = lax.axis_size(axis)
        spread = jnp.broadcast_to(total[None], (count,) + total.shape)
        total = jnp.sum(lax.all_to_all(spread, axis, 0, 0, tiled=True), axis=0)
    return total


def gather_params(weights, gains, first_row, last_row):
    latent = weights[0].shape[1]
    count = lax.axis_size("dom")
    index = lax.axis_index("dom")
    gain_row = gains.reshape(1, -1)
    gain_row = jnp.pad(gain_row, ((0, 0), (0, latent - gain_row.shape[1])))
    packed = jnp.concatenate(list(weights) + [gain_row], axis=0)
    target = jnp.arange(count)[:, None, None]
    edge_rows = jnp.where(target == index + 1, last_row[None], jnp.where(target == index - 1, first_row[None], 0))
    spread = jnp.concatenate(
        [jnp.broadcast_to(packed[None], (count,) + packed.shape), edge_rows.astype(packed.dtype)], axis=1
    )
    received = lax.all_to_all(spread, "dom", 0, 0, tiled=True)
    rows = packed.shape[0]
    top = lax.dynamic_index_in_dim(received, (index + count - 1) % count, keepdims=False)[rows:]
    bottom = lax.dynamic_index_in_dim(received, (index + 1) % count, keepdims=False)[rows:]
    full = received[:, :rows]
    outs = []
    start = 0
    for w in weights:
        part = w.shape[0]
        outs.append(full[:, start : start + part].reshape(count * part, latent))
        start += part
    width = gains.shape[1]
    gain_full = full[:, start, : 2 * width].reshape(count, 2, width)
    gain_full = jnp.transpose(gain_full, (1, 0, 2)).reshape(2, count * width)
    outs.append(gain_full)
    return tuple(outs), top, bottom


def reduce_params(parts, gain_terms, scale):
    count = lax.axis_size("dom")
    latent = parts[0].shape[1]
    blocks = [p.reshape(count, p.shape[0] // count, latent) for p in parts]
    width = gain_terms.shape[1] // count
    gain_block = jnp.transpose(gain_terms.reshape(2, count, width), (1, 0, 2)).reshape(count, 1, 2 * width)
    gain_block = jnp.pad(gain_block, ((0, 0), (0, 0), (0, latent - 2 * width)))
    packed = jnp.concatenate(blocks + [gain_block], axis=1)
    shard = reduce_scatter_dom(packed)
    shard = sum_sub(shard) * scale
    outs = []
    start = 0
    for b in blocks:
        rows = b.shape[1]
        outs.append(shard[start : start + rows])
        start += rows
    outs.append(shard[start, : 2 * width].reshape(2, width))
    return tuple(outs)


def shift_in(value, axis, step):
    count = axis_count(axis)
    if step > 0:
        pairs = [(i, i + 1) for i in range(count - 1)]
    else:
        pairs = [(i + 1, i) for i in range(count - 1)]
    return lax.ppermute(value.astype(jnp.bfloat16), axis, pairs).astype(value.dtype)


def one_hot(index, count):
    return (index[:, None] == jnp.arange(count, dtype=index.dtype)[None, :]).astype(jnp.bfloat16)


def select_rows(pick, table):
    if table.dtype == jnp.bfloat16:
        return jnp.dot(pick, table, preferred_element_type=jnp.float32).astype(jnp.bfloat16)
    return jnp.dot(
        pick.astype(jnp.float32), table, precision=lax.Precision.HIGHEST, preferred_element_type=jnp.float32
    )


def sum_rows(pick, values):
    return lax.dot_general(
        pick.astype(jnp.float32),
        values,
        (((0,), (0,)), ((), ())),
        precision=lax.Precision.HIGHEST,
        preferred_element_type=jnp.float32,
    )


def shards(
    node_feat,
    edge_feat,
    edge_dst,
    edge_dir,
    edge_count,
    w_edge_in,
    w_edge_out,
    w_node_in,
    w_node_out,
    gains,
    node_cot,
    edge_cot,
):
    (full_edge_in, full_edge_out, full_node_in, full_node_out, full_gains), top, bottom = gather_params(
        (w_edge_in, w_edge_out, w_node_in, w_node_out), gains, node_feat[0], node_feat[-1]
    )
    gain_edge = full_gains[0].astype(jnp.float32)
    gain_node = full_gains[1].astype(jnp.float32)
    block_side = node_feat.shape[0]
    latent = node_feat.shape[2]
    padded_side = block_side + 2
    left = shift_in(node_feat[:, -1], SUB, 1)
    right = shift_in(node_feat[:, 0], SUB, -1)
    middle = jnp.concatenate([left[:, None], node_feat, right[:, None]], axis=1)
    edge_rows = jnp.pad(jnp.stack([top, bottom]), ((0, 0), (1, 1), (0, 0)))
    padded = jnp.concatenate([edge_rows[:1], middle, edge_rows[1:]], axis=0).reshape(
        padded_side * padded_side, latent
    )
    node_row = edge_dst // block_side
    node_col = edge_dst % block_side
    step_row = jnp.where(edge_dir == 0, 1, jnp.where(edge_dir == 1, -1, 0)).astype(jnp.int32)
    step_col = jnp.where(edge_dir == 2, 1, jnp.where(edge_dir == 3, -1, 0)).astype(jnp.int32)
    target_pad = (node_row + 1) * padded_side + node_col + 1
    source_pad = (node_row + 1 + step_row) * padded_side + node_col + 1 + step_col
    active = (jnp.arange(edge_dst.shape[0], dtype=jnp.int32) < edge_count[0]).astype(jnp.float32)[
        :, None
    ]
    padded_count = padded_side * padded_side
    pick_source = one_hot(source_pad, padded_count)
    pick_target = one_hot(target_pad, padded_count)
    pick_local = one_hot(edge_dst, block_side * block_side)
    inputs = jnp.concatenate(
        [edge_feat, select_rows(pick_source, padded), select_rows(pick_target, padded)], axis=1
    )
    pre_e, hidden_e, normed_e, inv_e, message = mlp_forward(
        inputs, full_edge_in, full_edge_out, gain_edge
    )
    aggregate = sum_rows(pick_local, message * active)
    node_rows = node_feat.reshape(block_side * block_side, latent)
    node_input = jnp.concatenate([node_rows, aggregate.astype(jnp.bfloat16)], axis=1)
    pre_n, hidden_n, normed_n, inv_n, _ = mlp_forward(
        node_input, full_node_in, full_node_out, gain_node
    )
    node_upstream = node_cot.reshape(block_side * block_side, latent).astype(jnp.float32)
    node_in_grad, node_first, node_second, node_gain = mlp_backward(
        node_upstream,
        node_input,
        pre_n,
        hidden_n,
        normed_n,
        inv_n,
        gain_node,
        full_node_in,
        full_node_out,
    )
    cot_float = edge_cot.astype(jnp.float32)
    upstream = active * (cot_float + select_rows(pick_local, node_in_grad[:, latent:]))
    edge_in_grad, edge_first, edge_second, edge_gain = mlp_backward(
        upstream, inputs, pre_e, hidden_e, normed_e, inv_e, gain_edge, full_edge_in, full_edge_out
    )
    edge_grad = (cot_float + edge_in_grad[:, :latent]).astype(jnp.bfloat16)
    spread = sum_rows(
        jnp.concatenate([pick_source, pick_target], axis=0),
        jnp.concatenate([edge_in_grad[:, latent : 2 * latent], edge_in_grad[:, 2 * latent :]], axis=0),
    )
    spread = spread.reshape(padded_side, padded_side, latent)
    inner = spread[1:-1, 1:-1]
    from_prev_dom = shift_in(spread[-1, 1:-1], "dom", 1)
    from_next_dom = shift_in(spread[0, 1:-1], "dom", -1)
    from_prev_sub = shift_in(spread[1:-1, -1], SUB, 1)
    from_next_sub = shift_in(spread[1:-1, 0], SUB, -1)
    inner = inner.at[0].add(from_prev_dom).at[-1].add(from_next_dom)
    inner = inner.at[:, 0].add(from_prev_sub).at[:, -1].add(from_next_sub)
    node_total = node_upstream + node_in_grad[:, :latent]
    node_grad = (node_total.reshape(block_side, block_side, latent) + inner).astype(jnp.bfloat16)
    nodes_all = block_side * block_side * lax.axis_size("dom") * axis_count(SUB)
    grad_scale = lax.rsqrt(jnp.float32(nodes_all))
    results = reduce_params(
        (edge_first, edge_second, node_first, node_second), jnp.stack([edge_gain, node_gain]), grad_scale
    )
    return (node_grad, edge_grad) + results


def solution(mesh):
    in_specs = (
        P("dom", SUB, None),
        P(("dom",) + SUB, None),
        P(("dom",) + SUB),
        P(("dom",) + SUB),
        P(("dom",) + SUB),
        P("dom", None),
        P("dom", None),
        P("dom", None),
        P("dom", None),
        P(None, "dom"),
        P("dom", SUB, None),
        P(("dom",) + SUB, None),
    )
    out_specs = (
        P("dom", SUB, None),
        P(("dom",) + SUB, None),
        P("dom", None),
        P("dom", None),
        P("dom", None),
        P("dom", None),
        P(None, "dom"),
    )
    devices = mesh.devices
    low = 8 if devices.shape[1] % 8 == 0 else 1
    split = jax.sharding.Mesh(
        devices.reshape(devices.shape[0], devices.shape[1] // low, low), ("dom",) + SUB
    )
    return jax.shard_map(shards, mesh=split, in_specs=in_specs, out_specs=out_specs, check_vma=False)
```
